32 devices in a mesh: ctx: 4 (over y, x), dp: 4 (over z), tp: 2 (over core).
Axes of the slice: x: 2, y: 2, z: 4, core: 2. Of those that a mesh axis runs over, the one named last changes fastest.
Arguments:
- queries: bfloat16 [4, 512, 32, 128], P('dp', 'ctx', 'tp'), may hold values from -21 to 21
- keys: bfloat16 [4, 512, 4, 128], P('dp', 'ctx', 'tp'), may hold values from -6 to 6
- values: bfloat16 [4, 512, 4, 128], P('dp', 'ctx', 'tp'), may hold values from -6 to 6
- output_cotangent: bfloat16 [4, 512, 32, 128], P('dp', 'ctx', 'tp'), may hold values from -6 to 6
- features: bfloat16 [4, 512, 4096], P('dp', 'ctx'), may hold values from -60 to 60
- doc_lengths: int32 [4, 48], P('dp'), may hold values from 1 to 16, 512 in all within a row
- rope_num: int32 [64], replicated, may hold values from 1 to 40
- rope_den: int32 [64], replicated, may hold values from 1 to 8
- param: float32 [4096, 512], P('dp', 'tp'), may hold values from -0.4375 to 0.4375
- first_moment_state: float32 [4096, 512], P('dp', 'tp'), may hold values from -4 to 4
- second_moment_state: float32 [4096, 512], P('dp', 'tp'), may hold values from 0.05 to 1
Outputs:
- grad_queries: bfloat16 [4, 512, 32, 128], P('dp', 'ctx', 'tp')
- grad_keys: bfloat16 [4, 512, 4, 128], P('dp', 'ctx', 'tp')
- value_gradient: bfloat16 [4, 512, 4, 128], P('dp', 'ctx', 'tp')
- new_param: float32 [4096, 512], P('dp', 'tp')
- new_first: float32 [4096, 512], P('dp', 'tp')
- new_second: float32 [4096, 512], P('dp', 'tp')
The draws below stay inside these ranges and needn't reach their ends.
Inputs may be any that keep to these rules, and one draw needn't show every extreme that they name: `doc_lengths`: each row's 48 lengths sum to 512, and the largest of each row is exactly 16.
All inputs are finite; a program needn't handle non-finite values.
Results may differ from the reference program's by a relative error of at most 0.0064.
Values may be sent and summed in bfloat16 or wider, within the bound.
No kernel may reach another device: no remote copies, remote signals or barrier semaphores. Data moves between devices by JAX's collectives and lax.ppermute only.
A program may use at most 64 MiB of HBM per device.

```python
import math
import jax
import jax.numpy as jnp
import numpy as np
from jax import lax

HEAD_SIZE = 128
QUERY_HEADS = 32
KEY_VALUE_HEADS = 4
WINDOW_INPUTS = 4096
TOKENS_PER_SHARD = 128
DOCS = 48
SEQUENCE_TOKENS = 512
DOC_MOST = 16
STEPS = 1
N_CTX = 4
N_DP = 4


def shared_keys(key):
    array_shape = (N_DP, SEQUENCE_TOKENS, KEY_VALUE_HEADS, HEAD_SIZE)
    base = jax.random.truncated_normal(jax.random.fold_in(key, 101), -6.0, 6.0, array_shape, jnp.float32)
    return base


def draw_keys(key, part):
    base = shared_keys(key)
    return base.astype(jnp.bfloat16)


def draw_queries(key, part):
    array_shape = (N_DP, SEQUENCE_TOKENS, QUERY_HEADS, HEAD_SIZE)
    base = jax.random.truncated_normal(jax.random.fold_in(key, 104), -6.0, 6.0, array_shape, jnp.float32)
    return base.astype(jnp.bfloat16)


def draw_features(key, part):
    array_shape = (N_DP, SEQUENCE_TOKENS, WINDOW_INPUTS)
    ramp = jnp.arange(WINDOW_INPUTS, dtype=jnp.float32) / WINDOW_INPUTS
    rough = jax.random.uniform(jax.random.fold_in(key, 201), (WINDOW_INPUTS,), jnp.float32, 0.0, 1.0)
    column_scale = jnp.exp(math.log(10.0) * (0.5 * ramp + 0.5 * rough))
    base = jax.random.truncated_normal(jax.random.fold_in(key, 203), -6.0, 6.0, array_shape, jnp.float32)
    return (base * column_scale).astype(jnp.bfloat16)


def touch_ends(array, own_key, smallest, largest):
    extent = array.shape
    index_at = [jax.random.randint(jax.random.fold_in(own_key, axis), (), 0, extent[axis]) for axis in range(len(extent))]
    array = array.at[tuple(index_at)].set(smallest)
    longest = extent.index(max(extent))
    index_at[longest] = (index_at[longest] + 1) % extent[longest]
    return array.at[tuple(index_at)].set(largest)


def shard_levels(own_key, dims, cuts, least, top_value):
    def one(axis_at, blocks):
        steps = jax.random.uniform(jax.random.fold_in(jax.random.fold_in(own_key, 6), axis_at), (blocks,), jnp.float32, least / len(cuts), top_value / len(cuts))
        return jnp.repeat(jnp.exp(steps), dims[axis_at] // blocks).reshape((-1,) + (1,) * (len(dims) - axis_at - 1))

    gain = one(*cuts[0])
    for cut in cuts[1:]:
        gain = gain * one(*cut)
    return gain


def length_profile(amount, total, bound, skew):
    weights = [(1 << 20) // math.isqrt(rank ** skew) + 1 for rank in range(2, amount + 1)]
    spare, holding = total - bound - (amount - 1), [1] * (amount - 1)
    while spare > 0:
        free = [i for i in range(amount - 1) if holding[i] < bound]
        whole, budget = sum([weights[i] for i in free]), spare
        for i in free:
            more = min(bound - holding[i], max(1, budget * weights[i] // whole), spare)
            holding[i] = holding[i] + more
            spare = spare - more
    return np.array([bound] + holding)


def ragged_sizes(stream_key, number_of, total, most, lean):
    if number_of == 2:
        one = jax.random.randint(stream_key, (), max(1, total - most), min(most, total - 1) + 1)
        return jnp.stack([one, total - one])
    lengths = jnp.asarray(length_profile(number_of, total, most, lean), jnp.int32)
    pairs = (number_of - 1) // 2
    source_of, taker = lengths[1:1 + 2 * pairs:2], lengths[2:2 + 2 * pairs:2]
    room = jnp.minimum(source_of - 1, most - taker)
    moved = jax.random.randint(jax.random.fold_in(stream_key, 1), (pairs,), 0, 1 << 20) % (room + 1)
    lengths = lengths.at[1:1 + 2 * pairs:2].set(source_of - moved).at[2:2 + 2 * pairs:2].set(taker + moved)
    return lengths[jax.random.permutation(jax.random.fold_in(stream_key, 2), number_of)]


def centred(own_key, dims, deviation, reach, pieces=(), kind=jnp.bfloat16):
    values = jax.random.normal(own_key, dims, jnp.float32) * deviation
    if len(pieces) > 0:
        values = shard_levels(own_key, dims, pieces, -0.22, 0.18) * values
    return jnp.clip(values, min=-reach, max=reach).astype(kind)


def setup_inputs(seed: int = 0) -> dict:
    key_list = jax.random.split(jax.random.key(seed), 12)
    queries = draw_queries(jax.random.fold_in(key_list[11], 71), 0)
    keys = draw_keys(jax.random.fold_in(key_list[11], 71), 0)
    values = centred(key_list[2], (N_DP, SEQUENCE_TOKENS, KEY_VALUE_HEADS, HEAD_SIZE), 1.0, 6.0, ((0, 4), (1, 4), (2, 2)))
    output_cotangent = centred(key_list[3], (N_DP, SEQUENCE_TOKENS, QUERY_HEADS, HEAD_SIZE), 1.0, 6.0, ((0, 4), (1, 4), (2, 2)))
    features = draw_features(jax.random.fold_in(key_list[11], 71), 0)
    doc_lengths = jax.vmap(lambda own: ragged_sizes(own, DOCS, SEQUENCE_TOKENS, DOC_MOST, 2))(jax.random.split(key_list[5], N_DP)).reshape((N_DP, DOCS)).astype(jnp.int32)
    rope_num = touch_ends(jax.random.randint(key_list[6], (HEAD_SIZE // 2,), 1, 41), jax.random.fold_in(key_list[6], 1), 1, 40).astype(jnp.int32)
    rope_den = touch_ends(jax.random.randint(key_list[7], (HEAD_SIZE // 2,), 1, 9), jax.random.fold_in(key_list[7], 1), 1, 8).astype(jnp.int32)
    param = centred(key_list[8], (WINDOW_INPUTS, KEY_VALUE_HEADS * HEAD_SIZE), 0.03, 0.4375, ((0, 4), (1, 2)), jnp.float32)
    first_moment_state = centred(key_list[9], (WINDOW_INPUTS, KEY_VALUE_HEADS * HEAD_SIZE), 0.3, 4.0, ((0, 4), (1, 2)), jnp.float32)
    second_moment_state = jnp.clip(jnp.exp(math.log(1.0) - 2.9957323 * jax.random.uniform(key_list[10], (WINDOW_INPUTS, KEY_VALUE_HEADS * HEAD_SIZE), jnp.float32) ** shard_levels(key_list[10], (WINDOW_INPUTS, KEY_VALUE_HEADS * HEAD_SIZE), ((0, 4), (1, 2)), -0.2, 0.2)), 0.05, 1.0)
    return dict(queries=queries, keys=keys, values=values, output_cotangent=output_cotangent, features=features, doc_lengths=doc_lengths, rope_num=rope_num, rope_den=rope_den, param=param, first_moment_state=first_moment_state, second_moment_state=second_moment_state)


ROPE_BASE = 500000.0
NEG_FILL = -1e+30
CLIP_NORM = 1000.0
LEARN_RATE = 0.0001
DECAY_RATE = 0.1
BETA_ONE = 0.9
BETA_TWO = 0.95
ADAM_EPS = 1e-08
FIRST_FIX = 1.0 - 0.9 ** 10
SECOND_FIX = 1.0 - 0.95 ** 10

def doc_layout(lengths_row, token_index):
    doc_ends = jnp.cumsum(lengths_row).astype(jnp.int32)
    passed = doc_ends[None, :] <= token_index[:, None]
    doc_start = lax.optimization_barrier(jnp.max(jnp.where(passed, doc_ends[None, :], 0), axis=1)).astype(jnp.int32)
    doc_id = lax.optimization_barrier(jnp.sum(passed.astype(jnp.int32), axis=1)).astype(jnp.int32)
    return (doc_id, (token_index - doc_start).astype(jnp.float32))

def rope_tables(position, rope_num, rope_den, head_dim):
    expo = jnp.arange(head_dim // 2, dtype=jnp.float32) * (2.0 / head_dim)
    freq = jnp.exp(-math.log(ROPE_BASE) * expo) * rope_den.astype(jnp.float32) / rope_num.astype(jnp.float32)
    angle = position[:, None] * freq[None, :]
    cosine = jnp.concatenate([jnp.cos(angle), jnp.cos(angle)], axis=1)
    sine = jnp.concatenate([jnp.sin(angle), jnp.sin(angle)], axis=1)
    return (cosine[:, None, :], sine[:, None, :])

def rotate(vectors, cosine, sine):
    half = vectors.shape[-1] // 2
    turned = jnp.concatenate([-vectors[..., half:], vectors[..., :half]], axis=-1)
    return vectors * cosine + turned * sine

def unrotate(grads_in, cosine, sine):
    half = grads_in.shape[-1] // 2
    scaled = grads_in * sine
    turned = jnp.concatenate([scaled[..., half:], -scaled[..., :half]], axis=-1)
    return grads_in * cosine + turned

def adam_update(param, first_moment_state, second_moment_state, weight_gradient, grad_total):
    clip_factor = jnp.minimum(jnp.float32(1.0), CLIP_NORM / jnp.sqrt(grad_total))
    clipped = weight_gradient * clip_factor
    new_first = BETA_ONE * first_moment_state + (1.0 - BETA_ONE) * clipped
    new_second = BETA_TWO * second_moment_state + (1.0 - BETA_TWO) * clipped * clipped
    step_size = new_first / FIRST_FIX / (jnp.sqrt(new_second / SECOND_FIX) + ADAM_EPS)
    new_param = param - LEARN_RATE * (step_size + DECAY_RATE * param)
    return (new_param, new_first, new_second)

def one_sequence(queries, keys, values, output_cotangent, lengths_row, rope_num, rope_den):
    token_index = jnp.arange(SEQUENCE_TOKENS, dtype=jnp.int32)
    doc_id, position = doc_layout(lengths_row, token_index)
    cosine, sine = rope_tables(position, rope_num, rope_den, HEAD_SIZE)
    group_size = QUERY_HEADS // KEY_VALUE_HEADS
    scale = HEAD_SIZE ** (-0.5)
    rotated_query_rows = rotate(queries.astype(jnp.float32), cosine, sine).astype(jnp.bfloat16)
    rotated_key_rows = rotate(keys.astype(jnp.float32), cosine, sine).astype(jnp.bfloat16)
    margin_width = STEPS * TOKENS_PER_SHARD
    window = margin_width + TOKENS_PER_SHARD
    padded_keys = jnp.concatenate([jnp.zeros((margin_width, KEY_VALUE_HEADS, HEAD_SIZE), jnp.bfloat16), rotated_key_rows], axis=0)
    padded_values = jnp.concatenate([jnp.zeros((margin_width, KEY_VALUE_HEADS, HEAD_SIZE), jnp.bfloat16), values], axis=0)
    docs_pad = jnp.concatenate([jnp.zeros((margin_width,), jnp.int32), doc_id], axis=0)

    def block_step(carry, block_id):
        key_grad, val_grad = carry
        first_index = (block_id * TOKENS_PER_SHARD).astype(jnp.int32)
        query_block = lax.dynamic_slice_in_dim(rotated_query_rows, first_index, TOKENS_PER_SHARD, 0).reshape(TOKENS_PER_SHARD, KEY_VALUE_HEADS, group_size, HEAD_SIZE).astype(jnp.float32)
        gradient_block = lax.dynamic_slice_in_dim(output_cotangent, first_index, TOKENS_PER_SHARD, 0).reshape(TOKENS_PER_SHARD, KEY_VALUE_HEADS, group_size, HEAD_SIZE).astype(jnp.float32)
        k_win = lax.dynamic_slice_in_dim(padded_keys, first_index, window, 0).astype(jnp.float32)
        v_win = lax.dynamic_slice_in_dim(padded_values, first_index, window, 0).astype(jnp.float32)
        q_doc = lax.dynamic_slice_in_dim(doc_id, first_index, TOKENS_PER_SHARD, 0)
        k_doc = lax.dynamic_slice_in_dim(docs_pad, first_index, window, 0)
        q_index = first_index + jnp.arange(TOKENS_PER_SHARD, dtype=jnp.int32)
        k_index = first_index - margin_width + jnp.arange(window, dtype=jnp.int32)
        valid = (k_index[None, :] >= 0) & (k_index[None, :] <= q_index[:, None]) & (k_doc[None, :] == q_doc[:, None])
        scores = jnp.einsum('qhgd,khd->hgqk', query_block, k_win) * scale
        scores = jnp.where(valid, scores, NEG_FILL)
        row_top = lax.optimization_barrier(jnp.max(scores, axis=-1, keepdims=True))
        weights = jnp.where(valid, jnp.exp(scores - row_top), 0.0)
        probs = weights / lax.optimization_barrier(jnp.sum(weights, axis=-1, keepdims=True))
        probs_low = lax.optimization_barrier(probs.astype(jnp.bfloat16)).astype(jnp.float32)
        attn_out = jnp.einsum('hgqk,khd->qhgd', probs_low, v_win)
        delta = lax.optimization_barrier(jnp.sum(gradient_block * attn_out, axis=-1))
        dprobs = jnp.einsum('qhgd,khd->hgqk', gradient_block, v_win)
        dscores = probs * (dprobs - jnp.transpose(delta, (1, 2, 0))[..., None])
        dscores = lax.optimization_barrier(dscores.astype(jnp.bfloat16)).astype(jnp.float32)
        q_part = jnp.einsum('hgqk,khd->qhgd', dscores, k_win) * scale
        k_part = jnp.einsum('hgqk,qhgd->khd', dscores, query_block) * scale
        v_part = jnp.einsum('hgqk,qhgd->khd', probs_low, gradient_block)
        key_grad = lax.dynamic_update_slice_in_dim(key_grad, lax.dynamic_slice_in_dim(key_grad, first_index, window, 0) + k_part, first_index, 0)
        val_grad = lax.dynamic_update_slice_in_dim(val_grad, lax.dynamic_slice_in_dim(val_grad, first_index, window, 0) + v_part, first_index, 0)
        return ((key_grad, val_grad), q_part.reshape(TOKENS_PER_SHARD, QUERY_HEADS, HEAD_SIZE))
    initial_state = (jnp.zeros((SEQUENCE_TOKENS + margin_width, KEY_VALUE_HEADS, HEAD_SIZE), jnp.float32), jnp.zeros((SEQUENCE_TOKENS + margin_width, KEY_VALUE_HEADS, HEAD_SIZE), jnp.float32))
    (key_grad, val_grad), query_grad = lax.scan(block_step, initial_state, jnp.arange(N_CTX, dtype=jnp.int32))
    query_grad = query_grad.reshape(SEQUENCE_TOKENS, QUERY_HEADS, HEAD_SIZE)
    grad_q = unrotate(query_grad, cosine, sine).astype(jnp.bfloat16)
    grad_k = unrotate(key_grad[margin_width:], cosine, sine).astype(jnp.bfloat16)
    grad_v = val_grad[margin_width:].astype(jnp.bfloat16)
    return (grad_q, grad_k, grad_v)

def reference(queries, keys, values, output_cotangent, features, doc_lengths, rope_num, rope_den, param, first_moment_state, second_moment_state):

    def per_sequence(bundle):
        return one_sequence(bundle[0], bundle[1], bundle[2], bundle[3], bundle[4], rope_num, rope_den)
    grad_queries, grad_keys, value_gradient = lax.map(per_sequence, (queries, keys, values, output_cotangent, doc_lengths))
    weight_gradient = jnp.dot(features.reshape(-1, WINDOW_INPUTS).T, value_gradient.reshape(-1, KEY_VALUE_HEADS * HEAD_SIZE), preferred_element_type=jnp.float32)
    grad_total = jnp.sum(weight_gradient * weight_gradient)
    new_param, new_first, new_second = adam_update(param, first_moment_state, second_moment_state, weight_gradient, grad_total)
    return (grad_queries, grad_keys, value_gradient, new_param, new_first, new_second)
```

```python
from functools import reduce
import math

import jax
import jax.numpy as jnp
from jax import lax
from jax.sharding import PartitionSpec as P

ROPE_BASE = 500000.0
NEG_FILL = -1e30
CLIP_NORM = 1000.0
LEARN_RATE = 0.0001
DECAY_RATE = 0.1
BETA_ONE = 0.9
BETA_TWO = 0.95
ADAM_EPS = 1e-08
FIRST_FIX = 1.0 - 0.9**10
SECOND_FIX = 1.0 - 0.95**10


def shifted(array, axis, by):
    peers = lax.axis_size(axis)
    pairs = [(i, i + by) for i in range(peers) if 0 <= i + by < peers]
    return lax.ppermute(array, axis, pairs)


def doc_layout(lengths_row, token_index):
    doc_ends = jnp.cumsum(lengths_row)
    passed = doc_ends[None, :] <= token_index[:, None]
    doc_start = jnp.max(jnp.where(passed, doc_ends[None, :], 0), axis=1)
    doc_id = jnp.sum(passed.astype(jnp.int32), axis=1)
    return (doc_id, (token_index - doc_start).astype(jnp.float32))


def rope_tables(position, rope_num, rope_den, head_dim):
    expo = jnp.arange(head_dim // 2, dtype=jnp.float32) * (2.0 / head_dim)
    freq = (
        jnp.exp(-math.log(ROPE_BASE) * expo)
        * rope_den.astype(jnp.float32)
        / rope_num.astype(jnp.float32)
    )
    angle = position[:, None] * freq[None, :]
    cosine = jnp.concatenate([jnp.cos(angle), jnp.cos(angle)], axis=1)
    sine = jnp.concatenate([jnp.sin(angle), jnp.sin(angle)], axis=1)
    return (cosine[:, None, :], sine[:, None, :])


def rotate(vectors, cosine, sine):
    half = vectors.shape[-1] // 2
    turned = jnp.concatenate([-vectors[..., half:], vectors[..., :half]], axis=-1)
    return vectors * cosine + turned * sine


def unrotate(grads_in, cosine, sine):
    half = grads_in.shape[-1] // 2
    scaled = grads_in * sine
    turned = jnp.concatenate([scaled[..., half:], -scaled[..., :half]], axis=-1)
    return grads_in * cosine + turned


def adam_update(param, first_moment_state, second_moment_state, weight_gradient, grad_total):
    clip_factor = jnp.minimum(jnp.float32(1.0), CLIP_NORM / jnp.sqrt(grad_total))
    clipped = weight_gradient * clip_factor
    new_first = BETA_ONE * first_moment_state + (1.0 - BETA_ONE) * clipped
    new_second = BETA_TWO * second_moment_state + (1.0 - BETA_TWO) * clipped * clipped
    step_size = new_first / FIRST_FIX / (jnp.sqrt(new_second / SECOND_FIX) + ADAM_EPS)
    new_param = param - LEARN_RATE * (step_size + DECAY_RATE * param)
    return (new_param, new_first, new_second)


def local(
    queries,
    keys,
    values,
    output_cotangent,
    features,
    doc_lengths,
    rope_num,
    rope_den,
    param,
    first_moment_state,
    second_moment_state,
):
    tok_rows = queries.shape[1]
    head_count = queries.shape[2]
    head_dim = queries.shape[3]
    kv_count = keys.shape[2]
    group_size = head_count // kv_count
    n_ctx = lax.axis_size("ctx")
    place = lax.axis_index("ctx")
    seq_len = tok_rows * n_ctx
    doc_most = seq_len // 32
    reach = (doc_most + tok_rows - 2) // tok_rows
    scale = head_dim ** (-0.5)
    lengths_row = doc_lengths[0]
    own_index = place * tok_rows + jnp.arange(tok_rows, dtype=jnp.int32)
    own_doc, position = doc_layout(lengths_row, own_index)
    cosine, sine = rope_tables(position, rope_num, rope_den, head_dim)
    rotated_query_rows = rotate(queries[0].astype(jnp.float32), cosine, sine).astype(jnp.bfloat16)
    rotated_query_rows = rotated_query_rows.reshape(tok_rows, kv_count, group_size, head_dim)
    rotated_key_rows = rotate(keys[0].astype(jnp.float32), cosine, sine).astype(jnp.bfloat16)
    grad_out = output_cotangent[0].reshape(tok_rows, kv_count, group_size, head_dim)
    kv_pair = jnp.stack([rotated_key_rows, values[0]])
    pairs = [kv_pair]
    offset = 1
    kv_pair = shifted(kv_pair, "ctx", 1)
    pairs.append(kv_pair)
    masks = []
    for offset in range(reach + 1):
        key_index = (place - offset) * tok_rows + jnp.arange(tok_rows, dtype=jnp.int32)
        key_doc = doc_layout(lengths_row, key_index)[0]
        valid = (
            (key_index[None, :] >= 0)
            & (key_index[None, :] <= own_index[:, None])
            & (key_doc[None, :] == own_doc[:, None])
        )
        masks.append(valid)
    score_list = []
    for pair_in, valid_in in zip(pairs, masks):
        raw = (
            jnp.einsum(
                "qhgd,khd->hgqk", rotated_query_rows, pair_in[0], preferred_element_type=jnp.float32
            )
            * scale
        )
        score_list.append(jnp.where(valid_in, raw, NEG_FILL))
    row_top = reduce(
        jnp.maximum, [jnp.max(scores, axis=-1, keepdims=True) for scores in score_list]
    )
    weight_list = [
        jnp.where(valid_in, jnp.exp(scores - row_top), 0.0)
        for scores, valid_in in zip(score_list, masks)
    ]
    row_total = reduce(
        jnp.add, [jnp.sum(weights, axis=-1, keepdims=True) for weights in weight_list]
    )
    prob_list = [weights / row_total for weights in weight_list]
    low_list = [probs.astype(jnp.bfloat16) for probs in prob_list]
    attn_out = reduce(
        jnp.add,
        [
            jnp.einsum("hgqk,khd->qhgd", probs_low, pair_in[1], preferred_element_type=jnp.float32)
            for probs_low, pair_in in zip(low_list, pairs)
        ],
    )
    delta = jnp.einsum("qhgd,qhgd->hgq", grad_out.astype(jnp.float32), attn_out)[..., None]
    query_terms = []
    key_terms = []
    for pair_in, probs, probs_low, valid_in in zip(pairs, prob_list, low_list, masks):
        dprobs = jnp.einsum(
            "qhgd,khd->hgqk", grad_out, pair_in[1], preferred_element_type=jnp.float32
        )
        dscores = (probs * (dprobs - delta)).astype(jnp.bfloat16)
        q_part = (
            jnp.einsum("hgqk,khd->qhgd", dscores, pair_in[0], preferred_element_type=jnp.float32)
            * scale
        )
        k_part = (
            jnp.einsum(
                "hgqk,qhgd->khd", dscores, rotated_query_rows, preferred_element_type=jnp.float32
            )
            * scale
        )
        v_part = jnp.einsum(
            "hgqk,qhgd->khd", probs_low, grad_out, preferred_element_type=jnp.float32
        )
        q_part, kv_part = (q_part, jnp.stack([k_part, v_part]))
        query_terms.append(q_part)
        key_terms.append(kv_part)
    query_grad = reduce(jnp.add, query_terms)
    key_total = key_terms[reach]
    offset = 0
    key_total = (
        shifted(key_total.astype(jnp.bfloat16), "ctx", -1).astype(key_total.dtype)
        + key_terms[offset]
    )
    grad_q = unrotate(query_grad.reshape(tok_rows, head_count, head_dim), cosine, sine).astype(
        jnp.bfloat16
    )
    grad_k = unrotate(key_total[0], cosine, sine).astype(jnp.bfloat16)
    grad_v = key_total[1].astype(jnp.bfloat16)
    feats = features[0]
    width = feats.shape[1]
    value_flat = grad_v.reshape(tok_rows, kv_count * head_dim)
    own_rows = param.shape[0]
    n_dp = lax.axis_size("dp")
    piece_rows = own_rows // n_ctx
    spread = ("dp", "ctx")
    feat_cols = lax.all_to_all(
        feats.reshape(tok_rows, n_dp * n_ctx, piece_rows), spread, 1, 0, tiled=False
    )
    value_rows = lax.all_gather(value_flat, spread, axis=0, tiled=False)
    pieces = lax.dot_general(
        feat_cols.reshape(-1, piece_rows),
        value_rows.reshape(-1, kv_count * head_dim),
        (((0,), (0,)), ((), ())),
        preferred_element_type=jnp.float32,
    )
    norm_part = jnp.sum(pieces * pieces)
    grad_total = lax.psum(norm_part, ("ctx", "dp", "tp"))
    weight_gradient = lax.all_gather(pieces, "ctx", axis=0, tiled=True)
    new_param, new_first, new_second = adam_update(
        param, first_moment_state, second_moment_state, weight_gradient, grad_total
    )
    return (grad_q[None], grad_k[None], grad_v[None], new_param, new_first, new_second)


def solution(mesh):
    placed = (
        P("dp", "ctx", "tp", None),
        P("dp", "ctx", "tp", None),
        P("dp", "ctx", "tp", None),
        P("dp", "ctx", "tp", None),
        P("dp", "ctx", None),
        P("dp", None),
        P(),
        P(),
        P("dp", "tp"),
        P("dp", "tp"),
        P("dp", "tp"),
    )
    return jax.shard_map(
        local,
        mesh=mesh,
        in_specs=placed,
        out_specs=(
            P("dp", "ctx", "tp", None),
            P("dp", "ctx", "tp", None),
            P("dp", "ctx", "tp", None),
            P("dp", "tp"),
            P("dp", "tp"),
            P("dp", "tp"),
        ),
        check_vma=False,
    )
```

```python
from functools import reduce
import math

import jax
import jax.numpy as jnp
from jax import lax
from jax.sharding import PartitionSpec as P

ROPE_BASE = 500000.0
NEG_FILL = -1e30
CLIP_NORM = 1000.0
LEARN_RATE = 0.0001
DECAY_RATE = 0.1
BETA_ONE = 0.9
BETA_TWO = 0.95
ADAM_EPS = 1e-08
FIRST_FIX = 1.0 - 0.9**10
SECOND_FIX = 1.0 - 0.95**10


def shifted(array, axis, by):
    peers = lax.axis_size(axis)
    pairs = [(i, i + by) for i in range(peers) if 0 <= i + by < peers]
    return lax.ppermute(array, axis, pairs)


def spread_copy(array, axes):
    peers = lax.axis_size(axes)
    if peers * array.size * array.dtype.itemsize > (4 << 20):
        return lax.all_gather(array, axes, axis=0, tiled=False)
    stacked = jnp.broadcast_to(array[None], (peers,) + array.shape)
    return lax.all_to_all(stacked, axes, 0, 0, tiled=False)


def spread_sum(value, axes):
    peers = lax.axis_size(axes)
    if peers > 64:
        return lax.psum(value, axes)
    return jnp.sum(spread_copy(jnp.full((8, 128), value), axes)[:, 0, 0])


def doc_layout(lengths_row, token_index):
    doc_ends = jnp.cumsum(lengths_row)
    passed = doc_ends[None, :] <= token_index[:, None]
    doc_start = jnp.max(jnp.where(passed, doc_ends[None, :], 0), axis=1)
    doc_id = jnp.sum(passed.astype(jnp.int32), axis=1)
    return (doc_id, (token_index - doc_start).astype(jnp.float32))


def rope_tables(position, rope_num, rope_den, head_dim):
    expo = jnp.arange(head_dim // 2, dtype=jnp.float32) * (2.0 / head_dim)
    freq = (
        jnp.exp(-math.log(ROPE_BASE) * expo)
        * rope_den.astype(jnp.float32)
        / rope_num.astype(jnp.float32)
    )
    angle = position[:, None] * freq[None, :]
    cosine = jnp.concatenate([jnp.cos(angle), jnp.cos(angle)], axis=1)
    sine = jnp.concatenate([jnp.sin(angle), jnp.sin(angle)], axis=1)
    return (cosine[:, None, :], sine[:, None, :])


def rotate(vectors, cosine, sine):
    half = vectors.shape[-1] // 2
    turned = jnp.concatenate([-vectors[..., half:], vectors[..., :half]], axis=-1)
    return vectors * cosine + turned * sine


def unrotate(grads_in, cosine, sine):
    half = grads_in.shape[-1] // 2
    scaled = grads_in * sine
    turned = jnp.concatenate([scaled[..., half:], -scaled[..., :half]], axis=-1)
    return grads_in * cosine + turned


def adam_update(param, first_moment_state, second_moment_state, weight_gradient, grad_total):
    clip_factor = jnp.minimum(jnp.float32(1.0), CLIP_NORM / jnp.sqrt(grad_total))
    clipped = weight_gradient * clip_factor
    new_first = BETA_ONE * first_moment_state + (1.0 - BETA_ONE) * clipped
    new_second = BETA_TWO * second_moment_state + (1.0 - BETA_TWO) * clipped * clipped
    step_size = new_first / FIRST_FIX / (jnp.sqrt(new_second / SECOND_FIX) + ADAM_EPS)
    new_param = param - LEARN_RATE * (step_size + DECAY_RATE * param)
    return (new_param, new_first, new_second)


def local(
    queries,
    keys,
    values,
    output_cotangent,
    features,
    doc_lengths,
    rope_num,
    rope_den,
    param,
    first_moment_state,
    second_moment_state,
):
    tok_rows = queries.shape[1]
    head_count = queries.shape[2]
    head_dim = queries.shape[3]
    kv_count = keys.shape[2]
    group_size = head_count // kv_count
    n_ctx = lax.axis_size("ctx")
    place = lax.axis_index("ctx")
    seq_len = tok_rows * n_ctx
    doc_most = seq_len // 32
    reach = (doc_most + tok_rows - 2) // tok_rows
    scale = head_dim ** (-0.5)
    lengths_row = doc_lengths[0]
    own_index = place * tok_rows + jnp.arange(tok_rows, dtype=jnp.int32)
    own_doc, position = doc_layout(lengths_row, own_index)
    cosine, sine = rope_tables(position, rope_num, rope_den, head_dim)
    rotated_query_rows = rotate(queries[0].astype(jnp.float32), cosine, sine).astype(jnp.bfloat16)
    rotated_query_rows = rotated_query_rows.reshape(tok_rows, kv_count, group_size, head_dim)
    rotated_key_rows = rotate(keys[0].astype(jnp.float32), cosine, sine).astype(jnp.bfloat16)
    grad_out = output_cotangent[0].reshape(tok_rows, kv_count, group_size, head_dim)
    kv_pair = jnp.stack([rotated_key_rows, values[0]])
    pairs = [kv_pair]
    offset = 1
    kv_pair = shifted(kv_pair, "ctx", 1)
    pairs.append(kv_pair)
    masks = []
    for offset in range(reach + 1):
        key_index = (place - offset) * tok_rows + jnp.arange(tok_rows, dtype=jnp.int32)
        key_doc = doc_layout(lengths_row, key_index)[0]
        valid = (
            (key_index[None, :] >= 0)
            & (key_index[None, :] <= own_index[:, None])
            & (key_doc[None, :] == own_doc[:, None])
        )
        masks.append(valid)
    score_list = []
    for pair_in, valid_in in zip(pairs, masks):
        raw = (
            jnp.einsum(
                "qhgd,khd->hgqk", rotated_query_rows, pair_in[0], preferred_element_type=jnp.float32
            )
            * scale
        )
        score_list.append(jnp.where(valid_in, raw, NEG_FILL))
    row_top = reduce(
        jnp.maximum, [jnp.max(scores, axis=-1, keepdims=True) for scores in score_list]
    )
    weight_list = [
        jnp.where(valid_in, jnp.exp(scores - row_top), 0.0)
        for scores, valid_in in zip(score_list, masks)
    ]
    row_total = reduce(
        jnp.add, [jnp.sum(weights, axis=-1, keepdims=True) for weights in weight_list]
    )
    prob_list = [weights / row_total for weights in weight_list]
    low_list = [probs.astype(jnp.bfloat16) for probs in prob_list]
    attn_out = reduce(
        jnp.add,
        [
            jnp.einsum("hgqk,khd->qhgd", probs_low, pair_in[1], preferred_element_type=jnp.float32)
            for probs_low, pair_in in zip(low_list, pairs)
        ],
    )
    delta = jnp.einsum("qhgd,qhgd->hgq", grad_out.astype(jnp.float32), attn_out)[..., None]
    query_terms = []
    key_terms = []
    for pair_in, probs, probs_low, valid_in in zip(pairs, prob_list, low_list, masks):
        dprobs = jnp.einsum(
            "qhgd,khd->hgqk", grad_out, pair_in[1], preferred_element_type=jnp.float32
        )
        dscores = (probs * (dprobs - delta)).astype(jnp.bfloat16)
        q_part = (
            jnp.einsum("hgqk,khd->qhgd", dscores, pair_in[0], preferred_element_type=jnp.float32)
            * scale
        )
        k_part = (
            jnp.einsum(
                "hgqk,qhgd->khd", dscores, rotated_query_rows, preferred_element_type=jnp.float32
            )
            * scale
        )
        v_part = jnp.einsum(
            "hgqk,qhgd->khd", probs_low, grad_out, preferred_element_type=jnp.float32
        )
        q_part, kv_part = (q_part, jnp.stack([k_part, v_part]))
        query_terms.append(q_part)
        key_terms.append(kv_part)
    query_grad = reduce(jnp.add, query_terms)
    key_total = key_terms[reach]
    offset = 0
    key_total = (
        shifted(key_total.astype(jnp.bfloat16), "ctx", -1).astype(key_total.dtype)
        + key_terms[offset]
    )
    grad_q = unrotate(query_grad.reshape(tok_rows, head_count, head_dim), cosine, sine).astype(
        jnp.bfloat16
    )
    grad_k = unrotate(key_total[0], cosine, sine).astype(jnp.bfloat16)
    grad_v = key_total[1].astype(jnp.bfloat16)
    feats = features[0]
    width = feats.shape[1]
    value_flat = grad_v.reshape(tok_rows, kv_count * head_dim)
    own_rows = param.shape[0]
    n_dp = lax.axis_size("dp")
    piece_rows = own_rows // n_ctx
    spread = ("dp", "ctx")
    feat_cols = lax.all_to_all(
        feats.reshape(tok_rows, n_dp * n_ctx, piece_rows), spread, 1, 0, tiled=False
    )
    value_rows = spread_copy(value_flat, spread)
    pieces = lax.dot_general(
        feat_cols.reshape(-1, piece_rows),
        value_rows.reshape(-1, kv_count * head_dim),
        (((0,), (0,)), ((), ())),
        preferred_element_type=jnp.float32,
    )
    norm_part = jnp.sum(pieces * pieces)
    everyone = ("ctx", "dp", "tp")
    grad_total = spread_sum(norm_part, everyone)
    weight_gradient = spread_copy(pieces, "ctx").reshape(own_rows, pieces.shape[1])
    new_param, new_first, new_second = adam_update(
        param, first_moment_state, second_moment_state, weight_gradient, grad_total
    )
    return (grad_q[None], grad_k[None], grad_v[None], new_param, new_first, new_second)


def solution(mesh):
    placed = (
        P("dp", "ctx", "tp", None),
        P("dp", "ctx", "tp", None),
        P("dp", "ctx", "tp", None),
        P("dp", "ctx", "tp", None),
        P("dp", "ctx", None),
        P("dp", None),
        P(),
        P(),
        P("dp", "tp"),
        P("dp", "tp"),
        P("dp", "tp"),
    )
    return jax.shard_map(
        local,
        mesh=mesh,
        in_specs=placed,
        out_specs=(
            P("dp", "ctx", "tp", None),
            P("dp", "ctx", "tp", None),
            P("dp", "ctx", "tp", None),
            P("dp", "tp"),
            P("dp", "tp"),
            P("dp", "tp"),
        ),
        check_vma=False,
    )
```

```python
from functools import reduce
import math

import jax
import jax.numpy as jnp
from jax import lax
from jax.sharding import PartitionSpec as P

ROPE_BASE = 500000.0
NEG_FILL = -1e30
CLIP_NORM = 1000.0
LEARN_RATE = 0.0001
DECAY_RATE = 0.1
BETA_ONE = 0.9
BETA_TWO = 0.95
ADAM_EPS = 1e-08
FIRST_FIX = 1.0 - 0.9**10
SECOND_FIX = 1.0 - 0.95**10


def shifted(array, axis, by):
    peers = lax.axis_size(axis)
    pairs = [(i, i + by) for i in range(peers) if 0 <= i + by < peers]
    return lax.ppermute(array, axis, pairs)


def spread_copy(array, axes):
    peers = lax.axis_size(axes)
    if peers * array.size * array.dtype.itemsize > (4 << 20):
        return lax.all_gather(array, axes, axis=0, tiled=False)
    stacked = jnp.broadcast_to(array[None], (peers,) + array.shape)
    return lax.all_to_all(stacked, axes, 0, 0, tiled=False)


def ring_copy(array, axis):
    peers = lax.axis_size(axis)
    place = lax.axis_index(axis)
    rows = array.shape[0]
    out = jnp.zeros((peers * rows,) + array.shape[1:], array.dtype)
    out = lax.dynamic_update_slice_in_dim(out, array, place * rows, 0)
    for step in range(1, peers):
        moved = lax.ppermute(array, axis, [(i, (i + step) % peers) for i in range(peers)])
        out = lax.dynamic_update_slice_in_dim(out, moved, ((place - step) % peers) * rows, 0)
    return out


def spread_sum(value, axes):
    peers = lax.axis_size(axes)
    if peers > 64:
        return lax.psum(value, axes)
    return jnp.sum(spread_copy(jnp.full((8, 128), value), axes)[:, 0, 0])


def doc_layout(lengths_row, token_index):
    doc_ends = jnp.cumsum(lengths_row)
    passed = doc_ends[None, :] <= token_index[:, None]
    doc_start = jnp.max(jnp.where(passed, doc_ends[None, :], 0), axis=1)
    doc_id = jnp.sum(passed.astype(jnp.int32), axis=1)
    return (doc_id, (token_index - doc_start).astype(jnp.float32))


def rope_tables(position, rope_num, rope_den, head_dim):
    expo = jnp.arange(head_dim // 2, dtype=jnp.float32) * (2.0 / head_dim)
    freq = (
        jnp.exp(-math.log(ROPE_BASE) * expo)
        * rope_den.astype(jnp.float32)
        / rope_num.astype(jnp.float32)
    )
    angle = position[:, None] * freq[None, :]
    cosine = jnp.concatenate([jnp.cos(angle), jnp.cos(angle)], axis=1)
    sine = jnp.concatenate([jnp.sin(angle), jnp.sin(angle)], axis=1)
    return (cosine[:, None, :], sine[:, None, :])


def rotate(vectors, cosine, sine):
    half = vectors.shape[-1] // 2
    turned = jnp.concatenate([-vectors[..., half:], vectors[..., :half]], axis=-1)
    return vectors * cosine + turned * sine


def unrotate(grads_in, cosine, sine):
    half = grads_in.shape[-1] // 2
    scaled = grads_in * sine
    turned = jnp.concatenate([scaled[..., half:], -scaled[..., :half]], axis=-1)
    return grads_in * cosine + turned


def adam_update(param, first_moment_state, second_moment_state, weight_gradient, grad_total):
    clip_factor = jnp.minimum(jnp.float32(1.0), CLIP_NORM / jnp.sqrt(grad_total))
    clipped = weight_gradient * clip_factor
    new_first = BETA_ONE * first_moment_state + (1.0 - BETA_ONE) * clipped
    new_second = BETA_TWO * second_moment_state + (1.0 - BETA_TWO) * clipped * clipped
    step_size = new_first / FIRST_FIX / (jnp.sqrt(new_second / SECOND_FIX) + ADAM_EPS)
    new_param = param - LEARN_RATE * (step_size + DECAY_RATE * param)
    return (new_param, new_first, new_second)


def local(
    queries,
    keys,
    values,
    output_cotangent,
    features,
    doc_lengths,
    rope_num,
    rope_den,
    param,
    first_moment_state,
    second_moment_state,
):
    tok_rows = queries.shape[1]
    head_count = queries.shape[2]
    head_dim = queries.shape[3]
    kv_count = keys.shape[2]
    group_size = head_count // kv_count
    n_ctx = lax.axis_size("ctx")
    place = lax.axis_index("ctx")
    seq_len = tok_rows * n_ctx
    doc_most = seq_len // 32
    reach = (doc_most + tok_rows - 2) // tok_rows
    scale = head_dim ** (-0.5)
    lengths_row = doc_lengths[0]
    own_index = place * tok_rows + jnp.arange(tok_rows, dtype=jnp.int32)
    own_doc, position = doc_layout(lengths_row, own_index)
    cosine, sine = rope_tables(position, rope_num, rope_den, head_dim)
    rotated_query_rows = rotate(queries[0].astype(jnp.float32), cosine, sine).astype(jnp.bfloat16)
    rotated_query_rows = rotated_query_rows.reshape(tok_rows, kv_count, group_size, head_dim)
    rotated_key_rows = rotate(keys[0].astype(jnp.float32), cosine, sine).astype(jnp.bfloat16)
    grad_out = output_cotangent[0].reshape(tok_rows, kv_count, group_size, head_dim)
    kv_pair = jnp.stack([rotated_key_rows, values[0]])
    pairs = [kv_pair]
    offset = 1
    kv_pair = shifted(kv_pair, "ctx", 1)
    pairs.append(kv_pair)
    masks = []
    for offset in range(reach + 1):
        key_index = (place - offset) * tok_rows + jnp.arange(tok_rows, dtype=jnp.int32)
        key_doc = doc_layout(lengths_row, key_index)[0]
        valid = (
            (key_index[None, :] >= 0)
            & (key_index[None, :] <= own_index[:, None])
            & (key_doc[None, :] == own_doc[:, None])
        )
        masks.append(valid)
    score_list = []
    for pair_in, valid_in in zip(pairs, masks):
        raw = (
            jnp.einsum(
                "qhgd,khd->hgqk", rotated_query_rows, pair_in[0], preferred_element_type=jnp.float32
            )
            * scale
        )
        score_list.append(jnp.where(valid_in, raw, NEG_FILL))
    row_top = reduce(
        jnp.maximum, [jnp.max(scores, axis=-1, keepdims=True) for scores in score_list]
    )
    weight_list = [
        jnp.where(valid_in, jnp.exp(scores - row_top), 0.0)
        for scores, valid_in in zip(score_list, masks)
    ]
    row_total = reduce(
        jnp.add, [jnp.sum(weights, axis=-1, keepdims=True) for weights in weight_list]
    )
    prob_list = [weights / row_total for weights in weight_list]
    low_list = [probs.astype(jnp.bfloat16) for probs in prob_list]
    attn_out = reduce(
        jnp.add,
        [
            jnp.einsum("hgqk,khd->qhgd", probs_low, pair_in[1], preferred_element_type=jnp.float32)
            for probs_low, pair_in in zip(low_list, pairs)
        ],
    )
    delta = jnp.einsum("qhgd,qhgd->hgq", grad_out.astype(jnp.float32), attn_out)[..., None]
    query_terms = []
    key_terms = []
    for pair_in, probs, probs_low, valid_in in zip(pairs, prob_list, low_list, masks):
        dprobs = jnp.einsum(
            "qhgd,khd->hgqk", grad_out, pair_in[1], preferred_element_type=jnp.float32
        )
        dscores = (probs * (dprobs - delta)).astype(jnp.bfloat16)
        q_part = (
            jnp.einsum("hgqk,khd->qhgd", dscores, pair_in[0], preferred_element_type=jnp.float32)
            * scale
        )
        k_part = (
            jnp.einsum(
                "hgqk,qhgd->khd", dscores, rotated_query_rows, preferred_element_type=jnp.float32
            )
            * scale
        )
        v_part = jnp.einsum(
            "hgqk,qhgd->khd", probs_low, grad_out, preferred_element_type=jnp.float32
        )
        q_part, kv_part = (q_part, jnp.stack([k_part, v_part]))
        query_terms.append(q_part)
        key_terms.append(kv_part)
    query_grad = reduce(jnp.add, query_terms)
    key_total = key_terms[reach]
    offset = 0
    key_total = (
        shifted(key_total.astype(jnp.bfloat16), "ctx", -1).astype(key_total.dtype)
        + key_terms[offset]
    )
    grad_q = unrotate(query_grad.reshape(tok_rows, head_count, head_dim), cosine, sine).astype(
        jnp.bfloat16
    )
    grad_k = unrotate(key_total[0], cosine, sine).astype(jnp.bfloat16)
    grad_v = key_total[1].astype(jnp.bfloat16)
    feats = features[0]
    width = feats.shape[1]
    value_flat = grad_v.reshape(tok_rows, kv_count * head_dim)
    own_rows = param.shape[0]
    n_dp = lax.axis_size("dp")
    piece_rows = own_rows // n_ctx
    spread = ("dp", "ctx")
    feat_cols = lax.all_to_all(
        feats.reshape(tok_rows, n_dp * n_ctx, piece_rows), spread, 1, 0, tiled=False
    )
    value_rows = spread_copy(value_flat, spread)
    pieces = lax.dot_general(
        feat_cols.reshape(-1, piece_rows),
        value_rows.reshape(-1, kv_count * head_dim),
        (((0,), (0,)), ((), ())),
        preferred_element_type=jnp.float32,
    )
    weight_gradient = ring_copy(pieces, "ctx")
    norm_part = jnp.sum(pieces * pieces)
    everyone = ("ctx", "dp", "tp")
    grad_total = spread_sum(norm_part, everyone)
    new_param, new_first, new_second = adam_update(
        param, first_moment_state, second_moment_state, weight_gradient, grad_total
    )
    return (grad_q[None], grad_k[None], grad_v[None], new_param, new_first, new_second)


def solution(mesh):
    placed = (
        P("dp", "ctx", "tp", None),
        P("dp", "ctx", "tp", None),
        P("dp", "ctx", "tp", None),
        P("dp", "ctx", "tp", None),
        P("dp", "ctx", None),
        P("dp", None),
        P(),
        P(),
        P("dp", "tp"),
        P("dp", "tp"),
        P("dp", "tp"),
    )
    return jax.shard_map(
        local,
        mesh=mesh,
        in_specs=placed,
        out_specs=(
            P("dp", "ctx", "tp", None),
            P("dp", "ctx", "tp", None),
            P("dp", "ctx", "tp", None),
            P("dp", "tp"),
            P("dp", "tp"),
            P("dp", "tp"),
        ),
        check_vma=False,
    )
```

```python
from functools import reduce
import math

import jax
import jax.numpy as jnp
from jax import lax
from jax.sharding import PartitionSpec as P

ROPE_BASE = 500000.0
NEG_FILL = -1e30
CLIP_NORM = 1000.0
LEARN_RATE = 0.0001
DECAY_RATE = 0.1
BETA_ONE = 0.9
BETA_TWO = 0.95
ADAM_EPS = 1e-08
FIRST_FIX = 1.0 - 0.9**10
SECOND_FIX = 1.0 - 0.95**10


def shifted(array, axis, by):
    peers = lax.axis_size(axis)
    pairs = [(i, i + by) for i in range(peers) if 0 <= i + by < peers]
    return lax.ppermute(array, axis, pairs)


def spread_copy(array, axes):
    peers = lax.axis_size(axes)
    if peers * array.size * array.dtype.itemsize > (4 << 20):
        return lax.all_gather(array, axes, axis=0, tiled=False)
    stacked = jnp.broadcast_to(array[None], (peers,) + array.shape)
    return lax.all_to_all(stacked, axes, 0, 0, tiled=False)


def ring_copy(array, axis):
    peers = lax.axis_size(axis)
    place = lax.axis_index(axis)
    rows = array.shape[0]
    out = jnp.zeros((peers * rows,) + array.shape[1:], array.dtype)
    out = lax.dynamic_update_slice_in_dim(out, array, place * rows, 0)
    for step in range(1, peers):
        moved = lax.ppermute(array, axis, [(i, (i + step) % peers) for i in range(peers)])
        out = lax.dynamic_update_slice_in_dim(out, moved, ((place - step) % peers) * rows, 0)
    return out


def spread_sum(value, axes):
    peers = lax.axis_size(axes)
    if peers > 64:
        return lax.psum(value, axes)
    return jnp.sum(spread_copy(jnp.full((8, 128), value), axes)[:, 0, 0])


def doc_layout(lengths_row, token_index):
    doc_ends = jnp.cumsum(lengths_row)
    passed = doc_ends[None, :] <= token_index[:, None]
    doc_start = jnp.max(jnp.where(passed, doc_ends[None, :], 0), axis=1)
    doc_id = jnp.sum(passed.astype(jnp.int32), axis=1)
    return (doc_id, (token_index - doc_start).astype(jnp.float32))


def rope_tables(position, rope_num, rope_den, head_dim):
    expo = jnp.arange(head_dim // 2, dtype=jnp.float32) * (2.0 / head_dim)
    freq = (
        jnp.exp(-math.log(ROPE_BASE) * expo)
        * rope_den.astype(jnp.float32)
        / rope_num.astype(jnp.float32)
    )
    angle = position[:, None] * freq[None, :]
    cosine = jnp.concatenate([jnp.cos(angle), jnp.cos(angle)], axis=1)
    sine = jnp.concatenate([jnp.sin(angle), jnp.sin(angle)], axis=1)
    return (cosine[:, None, :], sine[:, None, :])


def rotate(vectors, cosine, sine):
    half = vectors.shape[-1] // 2
    turned = jnp.concatenate([-vectors[..., half:], vectors[..., :half]], axis=-1)
    return vectors * cosine + turned * sine


def unrotate(grads_in, cosine, sine):
    half = grads_in.shape[-1] // 2
    scaled = grads_in * sine
    turned = jnp.concatenate([scaled[..., half:], -scaled[..., :half]], axis=-1)
    return grads_in * cosine + turned


def adam_update(param, first_moment_state, second_moment_state, weight_gradient, grad_total):
    clip_factor = jnp.minimum(jnp.float32(1.0), CLIP_NORM / jnp.sqrt(grad_total))
    clipped = weight_gradient * clip_factor
    new_first = BETA_ONE * first_moment_state + (1.0 - BETA_ONE) * clipped
    new_second = BETA_TWO * second_moment_state + (1.0 - BETA_TWO) * clipped * clipped
    step_size = new_first / FIRST_FIX / (jnp.sqrt(new_second / SECOND_FIX) + ADAM_EPS)
    new_param = param - LEARN_RATE * (step_size + DECAY_RATE * param)
    return (new_param, new_first, new_second)


def local(
    queries,
    keys,
    values,
    output_cotangent,
    features,
    doc_lengths,
    rope_num,
    rope_den,
    param,
    first_moment_state,
    second_moment_state,
):
    tok_rows = queries.shape[1]
    head_count = queries.shape[2]
    head_dim = queries.shape[3]
    kv_count = keys.shape[2]
    group_size = head_count // kv_count
    n_ctx = lax.axis_size("ctx")
    place = lax.axis_index("ctx")
    seq_len = tok_rows * n_ctx
    doc_most = seq_len // 32
    reach = (doc_most + tok_rows - 2) // tok_rows
    scale = head_dim ** (-0.5)
    lengths_row = doc_lengths[0]
    own_index = place * tok_rows + jnp.arange(tok_rows, dtype=jnp.int32)
    own_doc, position = doc_layout(lengths_row, own_index)
    cosine, sine = rope_tables(position, rope_num, rope_den, head_dim)
    rotated_query_rows = rotate(queries[0].astype(jnp.float32), cosine, sine).astype(jnp.bfloat16)
    rotated_query_rows = rotated_query_rows.reshape(tok_rows, kv_count, group_size, head_dim)
    rotated_key_rows = rotate(keys[0].astype(jnp.float32), cosine, sine).astype(jnp.bfloat16)
    grad_out = output_cotangent[0].reshape(tok_rows, kv_count, group_size, head_dim)
    kv_pair = jnp.stack([rotated_key_rows, values[0]])
    pairs = [kv_pair]
    offset = 1
    kv_pair = shifted(kv_pair, "ctx", 1)
    pairs.append(kv_pair)
    masks = []
    for offset in range(reach + 1):
        key_index = (place - offset) * tok_rows + jnp.arange(tok_rows, dtype=jnp.int32)
        key_doc = doc_layout(lengths_row, key_index)[0]
        valid = (
            (key_index[None, :] >= 0)
            & (key_index[None, :] <= own_index[:, None])
            & (key_doc[None, :] == own_doc[:, None])
        )
        masks.append(valid)
    score_list = []
    for pair_in, valid_in in zip(pairs, masks):
        raw = (
            jnp.einsum(
                "qhgd,khd->hgqk", rotated_query_rows, pair_in[0], preferred_element_type=jnp.float32
            )
            * scale
        )
        score_list.append(jnp.where(valid_in, raw, NEG_FILL))
    row_top = reduce(
        jnp.maximum, [jnp.max(scores, axis=-1, keepdims=True) for scores in score_list]
    )
    weight_list = [
        jnp.where(valid_in, jnp.exp(scores - row_top), 0.0)
        for scores, valid_in in zip(score_list, masks)
    ]
    row_total = reduce(
        jnp.add, [jnp.sum(weights, axis=-1, keepdims=True) for weights in weight_list]
    )
    prob_list = [weights / row_total for weights in weight_list]
    low_list = [probs.astype(jnp.bfloat16) for probs in prob_list]
    attn_out = reduce(
        jnp.add,
        [
            jnp.einsum("hgqk,khd->qhgd", probs_low, pair_in[1], preferred_element_type=jnp.float32)
            for probs_low, pair_in in zip(low_list, pairs)
        ],
    )
    delta = jnp.einsum("qhgd,qhgd->hgq", grad_out.astype(jnp.float32), attn_out)[..., None]
    value_terms = [
        jnp.einsum("hgqk,qhgd->khd", probs_low, grad_out, preferred_element_type=jnp.float32)
        for probs_low in low_list
    ]
    value_total = (
        shifted(value_terms[reach].astype(jnp.bfloat16), "ctx", -1).astype(jnp.float32)
        + value_terms[0]
    )
    grad_v = value_total.astype(jnp.bfloat16)
    query_terms = []
    key_terms = []
    for pair_in, probs, valid_in in zip(pairs, prob_list, masks):
        dprobs = jnp.einsum(
            "qhgd,khd->hgqk", grad_out, pair_in[1], preferred_element_type=jnp.float32
        )
        dscores = (probs * (dprobs - delta)).astype(jnp.bfloat16)
        q_part = (
            jnp.einsum("hgqk,khd->qhgd", dscores, pair_in[0], preferred_element_type=jnp.float32)
            * scale
        )
        k_part = (
            jnp.einsum(
                "hgqk,qhgd->khd", dscores, rotated_query_rows, preferred_element_type=jnp.float32
            )
            * scale
        )
        query_terms.append(q_part)
        key_terms.append(k_part)
    query_grad = reduce(jnp.add, query_terms)
    key_total = (
        shifted(key_terms[reach].astype(jnp.bfloat16), "ctx", -1).astype(jnp.float32)
        + key_terms[0]
    )
    grad_q = unrotate(query_grad.reshape(tok_rows, head_count, head_dim), cosine, sine).astype(
        jnp.bfloat16
    )
    grad_k = unrotate(key_total, cosine, sine).astype(jnp.bfloat16)
    feats = features[0]
    width = feats.shape[1]
    value_flat = grad_v.reshape(tok_rows, kv_count * head_dim)
    own_rows = param.shape[0]
    n_dp = lax.axis_size("dp")
    piece_rows = own_rows // n_ctx
    spread = ("dp", "ctx")
    feat_cols = lax.all_to_all(
        feats.reshape(tok_rows, n_dp * n_ctx, piece_rows), spread, 1, 0, tiled=False
    )
    value_rows = spread_copy(value_flat, spread)
    pieces = lax.dot_general(
        feat_cols.reshape(-1, piece_rows),
        value_rows.reshape(-1, kv_count * head_dim),
        (((0,), (0,)), ((), ())),
        preferred_element_type=jnp.float32,
    )
    weight_gradient = ring_copy(pieces, "ctx")
    norm_part = jnp.sum(pieces * pieces)
    everyone = ("ctx", "dp", "tp")
    grad_total = spread_sum(norm_part, everyone)
    new_param, new_first, new_second = adam_update(
        param, first_moment_state, second_moment_state, weight_gradient, grad_total
    )
    return (grad_q[None], grad_k[None], grad_v[None], new_param, new_first, new_second)


def solution(mesh):
    placed = (
        P("dp", "ctx", "tp", None),
        P("dp", "ctx", "tp", None),
        P("dp", "ctx", "tp", None),
        P("dp", "ctx", "tp", None),
        P("dp", "ctx", None),
        P("dp", None),
        P(),
        P(),
        P("dp", "tp"),
        P("dp", "tp"),
        P("dp", "tp"),
    )
    return jax.shard_map(
        local,
        mesh=mesh,
        in_specs=placed,
        out_specs=(
            P("dp", "ctx", "tp", None),
            P("dp", "ctx", "tp", None),
            P("dp", "ctx", "tp", None),
            P("dp", "tp"),
            P("dp", "tp"),
            P("dp", "tp"),
        ),
        check_vma=False,
    )
```

```python
from functools import reduce
import math

import jax
import jax.numpy as jnp
from jax import lax
from jax.sharding import PartitionSpec as P

ROPE_BASE = 500000.0
NEG_FILL = -1e30
CLIP_NORM = 1000.0
LEARN_RATE = 0.0001
DECAY_RATE = 0.1
BETA_ONE = 0.9
BETA_TWO = 0.95
ADAM_EPS = 1e-08
FIRST_FIX = 1.0 - 0.9**10
SECOND_FIX = 1.0 - 0.95**10


def shifted(array, axis, by):
    peers = lax.axis_size(axis)
    pairs = [(i, i + by) for i in range(peers) if 0 <= i + by < peers]
    return lax.ppermute(array, axis, pairs)


def spread_copy(array, axes):
    peers = lax.axis_size(axes)
    if peers * array.size * array.dtype.itemsize > (4 << 20):
        return lax.all_gather(array, axes, axis=0, tiled=False)
    stacked = jnp.broadcast_to(array[None], (peers,) + array.shape)
    return lax.all_to_all(stacked, axes, 0, 0, tiled=False)


def ring_copy(array, axis):
    peers = lax.axis_size(axis)
    place = lax.axis_index(axis)
    rows = array.shape[0]
    out = jnp.zeros((peers * rows,) + array.shape[1:], array.dtype)
    out = lax.dynamic_update_slice_in_dim(out, array, place * rows, 0)
    for step in range(1, peers):
        moved = lax.ppermute(array, axis, [(i, (i + step) % peers) for i in range(peers)])
        out = lax.dynamic_update_slice_in_dim(out, moved, ((place - step) % peers) * rows, 0)
    return out


def spread_sum(value, axes):
    peers = lax.axis_size(axes)
    if peers > 64:
        return lax.psum(value, axes)
    return jnp.sum(spread_copy(jnp.full((8, 128), value), axes)[:, 0, 0])


def doc_layout(lengths_row, token_index):
    doc_ends = jnp.cumsum(lengths_row)
    passed = doc_ends[None, :] <= token_index[:, None]
    doc_start = jnp.max(jnp.where(passed, doc_ends[None, :], 0), axis=1)
    doc_id = jnp.sum(passed.astype(jnp.int32), axis=1)
    return (doc_id, (token_index - doc_start).astype(jnp.float32))


def rope_tables(position, rope_num, rope_den, head_dim):
    expo = jnp.arange(head_dim // 2, dtype=jnp.float32) * (2.0 / head_dim)
    freq = (
        jnp.exp(-math.log(ROPE_BASE) * expo)
        * rope_den.astype(jnp.float32)
        / rope_num.astype(jnp.float32)
    )
    angle = position[:, None] * freq[None, :]
    cosine = jnp.concatenate([jnp.cos(angle), jnp.cos(angle)], axis=1)
    sine = jnp.concatenate([jnp.sin(angle), jnp.sin(angle)], axis=1)
    return (cosine[:, None, :], sine[:, None, :])


def rotate(vectors, cosine, sine):
    half = vectors.shape[-1] // 2
    turned = jnp.concatenate([-vectors[..., half:], vectors[..., :half]], axis=-1)
    return vectors * cosine + turned * sine


def unrotate(grads_in, cosine, sine):
    half = grads_in.shape[-1] // 2
    scaled = grads_in * sine
    turned = jnp.concatenate([scaled[..., half:], -scaled[..., :half]], axis=-1)
    return grads_in * cosine + turned


def adam_update(param, first_moment_state, second_moment_state, weight_gradient, grad_total):
    clip_factor = jnp.minimum(jnp.float32(1.0), CLIP_NORM / jnp.sqrt(grad_total))
    clipped = weight_gradient * clip_factor
    new_first = BETA_ONE * first_moment_state + (1.0 - BETA_ONE) * clipped
    new_second = BETA_TWO * second_moment_state + (1.0 - BETA_TWO) * clipped * clipped
    step_size = new_first / FIRST_FIX / (jnp.sqrt(new_second / SECOND_FIX) + ADAM_EPS)
    new_param = param - LEARN_RATE * (step_size + DECAY_RATE * param)
    return (new_param, new_first, new_second)


def local(
    queries,
    keys,
    values,
    output_cotangent,
    features,
    doc_lengths,
    rope_num,
    rope_den,
    param,
    first_moment_state,
    second_moment_state,
):
    tok_rows = queries.shape[1]
    head_count = queries.shape[2]
    head_dim = queries.shape[3]
    kv_count = keys.shape[2]
    group_size = head_count // kv_count
    n_ctx = lax.axis_size("ctx")
    place = lax.axis_index("ctx")
    seq_len = tok_rows * n_ctx
    doc_most = seq_len // 32
    reach = (doc_most + tok_rows - 2) // tok_rows
    scale = head_dim ** (-0.5)
    lengths_row = doc_lengths[0]
    own_index = place * tok_rows + jnp.arange(tok_rows, dtype=jnp.int32)
    own_doc, position = doc_layout(lengths_row, own_index)
    cosine, sine = rope_tables(position, rope_num, rope_den, head_dim)
    rotated_query_rows = rotate(queries[0].astype(jnp.float32), cosine, sine).astype(jnp.bfloat16)
    rotated_query_rows = rotated_query_rows.reshape(tok_rows, kv_count, group_size, head_dim)
    rotated_key_rows = rotate(keys[0].astype(jnp.float32), cosine, sine).astype(jnp.bfloat16)
    grad_out = output_cotangent[0].reshape(tok_rows, kv_count, group_size, head_dim)
    kv_pair = jnp.stack([rotated_key_rows, values[0]])
    pairs = [kv_pair]
    offset = 1
    kv_pair = shifted(kv_pair, "ctx", 1)
    pairs.append(kv_pair)
    masks = []
    for offset in range(reach + 1):
        key_index = (place - offset) * tok_rows + jnp.arange(tok_rows, dtype=jnp.int32)
        key_doc = doc_layout(lengths_row, key_index)[0]
        valid = (
            (key_index[None, :] >= 0)
            & (key_index[None, :] <= own_index[:, None])
            & (key_doc[None, :] == own_doc[:, None])
        )
        masks.append(valid)
    score_list = []
    for pair_in, valid_in in zip(pairs, masks):
        raw = (
            jnp.einsum(
                "qhgd,khd->hgqk", rotated_query_rows, pair_in[0], preferred_element_type=jnp.float32
            )
            * scale
        )
        score_list.append(jnp.where(valid_in, raw, NEG_FILL))
    row_top = reduce(
        jnp.maximum, [jnp.max(scores, axis=-1, keepdims=True) for scores in score_list]
    )
    weight_list = [
        jnp.where(valid_in, jnp.exp(scores - row_top), 0.0)
        for scores, valid_in in zip(score_list, masks)
    ]
    row_total = reduce(
        jnp.add, [jnp.sum(weights, axis=-1, keepdims=True) for weights in weight_list]
    )
    prob_list = [weights / row_total for weights in weight_list]
    low_list = [probs.astype(jnp.bfloat16) for probs in prob_list]
    attn_out = reduce(
        jnp.add,
        [
            jnp.einsum("hgqk,khd->qhgd", probs_low, pair_in[1], preferred_element_type=jnp.float32)
            for probs_low, pair_in in zip(low_list, pairs)
        ],
    )
    delta = jnp.einsum("qhgd,qhgd->hgq", grad_out.astype(jnp.float32), attn_out)[..., None]
    value_terms = [
        jnp.einsum("hgqk,qhgd->khd", probs_low, grad_out, preferred_element_type=jnp.float32)
        for probs_low in low_list
    ]
    value_total = (
        shifted(value_terms[reach].astype(jnp.bfloat16), "ctx", -1).astype(jnp.float32)
        + value_terms[0]
    )
    grad_v = value_total.astype(jnp.bfloat16)
    query_terms = []
    key_terms = []
    for pair_in, probs, valid_in in zip(pairs, prob_list, masks):
        dprobs = jnp.einsum(
            "qhgd,khd->hgqk", grad_out, pair_in[1], preferred_element_type=jnp.float32
        )
        dscores = (probs * (dprobs - delta)).astype(jnp.bfloat16)
        q_part = (
            jnp.einsum("hgqk,khd->qhgd", dscores, pair_in[0], preferred_element_type=jnp.float32)
            * scale
        )
        k_part = (
            jnp.einsum(
                "hgqk,qhgd->khd", dscores, rotated_query_rows, preferred_element_type=jnp.float32
            )
            * scale
        )
        query_terms.append(q_part)
        key_terms.append(k_part)
    query_grad = reduce(jnp.add, query_terms)
    key_total = (
        shifted(key_terms[reach].astype(jnp.bfloat16), "ctx", -1).astype(jnp.float32)
        + key_terms[0]
    )
    grad_q = unrotate(query_grad.reshape(tok_rows, head_count, head_dim), cosine, sine).astype(
        jnp.bfloat16
    )
    grad_k = unrotate(key_total, cosine, sine).astype(jnp.bfloat16)
    feats = features[0]
    width = feats.shape[1]
    value_flat = grad_v.reshape(tok_rows, kv_count * head_dim)
    own_rows = param.shape[0]
    n_dp = lax.axis_size("dp")
    piece_rows = own_rows // n_ctx
    feat_cols = lax.all_to_all(
        feats.reshape(tok_rows, n_dp, n_ctx, piece_rows), "ctx", 2, 0, tiled=False
    )
    value_rows = spread_copy(value_flat, "ctx")
    partials = lax.dot_general(
        feat_cols.reshape(n_ctx * tok_rows, n_dp * piece_rows),
        value_rows.reshape(n_ctx * tok_rows, kv_count * head_dim),
        (((0,), (0,)), ((), ())),
        preferred_element_type=jnp.float32,
    ).reshape(n_dp, piece_rows, kv_count * head_dim)
    pieces = jnp.sum(lax.all_to_all(partials, "dp", 0, 0, tiled=False), axis=0)
    weight_gradient = ring_copy(pieces, "ctx")
    norm_part = jnp.sum(pieces * pieces)
    everyone = ("ctx", "dp", "tp")
    grad_total = spread_sum(norm_part, everyone)
    new_param, new_first, new_second = adam_update(
        param, first_moment_state, second_moment_state, weight_gradient, grad_total
    )
    return (grad_q[None], grad_k[None], grad_v[None], new_param, new_first, new_second)


def solution(mesh):
    placed = (
        P("dp", "ctx", "tp", None),
        P("dp", "ctx", "tp", None),
        P("dp", "ctx", "tp", None),
        P("dp", "ctx", "tp", None),
        P("dp", "ctx", None),
        P("dp", None),
        P(),
        P(),
        P("dp", "tp"),
        P("dp", "tp"),
        P("dp", "tp"),
    )
    return jax.shard_map(
        local,
        mesh=mesh,
        in_specs=placed,
        out_specs=(
            P("dp", "ctx", "tp", None),
            P("dp", "ctx", "tp", None),
            P("dp", "ctx", "tp", None),
            P("dp", "tp"),
            P("dp", "tp"),
            P("dp", "tp"),
        ),
        check_vma=False,
    )
```

```python
from functools import reduce
import math

import jax
import jax.numpy as jnp
from jax import lax
from jax.sharding import PartitionSpec as P

ROPE_BASE = 500000.0
NEG_FILL = -1e30
CLIP_NORM = 1000.0
LEARN_RATE = 0.0001
DECAY_RATE = 0.1
BETA_ONE = 0.9
BETA_TWO = 0.95
ADAM_EPS = 1e-08
FIRST_FIX = 1.0 - 0.9**10
SECOND_FIX = 1.0 - 0.95**10


def shifted(array, axis, by):
    peers = lax.axis_size(axis)
    pairs = [(i, i + by) for i in range(peers) if 0 <= i + by < peers]
    return lax.ppermute(array, axis, pairs)


def spread_copy(array, axes):
    peers = lax.axis_size(axes)
    if peers * array.size * array.dtype.itemsize > (4 << 20):
        return lax.all_gather(array, axes, axis=0, tiled=False)
    stacked = jnp.broadcast_to(array[None], (peers,) + array.shape)
    return lax.all_to_all(stacked, axes, 0, 0, tiled=False)


def ring_copy(array, axis):
    peers = lax.axis_size(axis)
    place = lax.axis_index(axis)
    rows = array.shape[0]
    out = jnp.zeros((peers * rows,) + array.shape[1:], array.dtype)
    out = lax.dynamic_update_slice_in_dim(out, array, place * rows, 0)
    for step in range(1, peers):
        moved = lax.ppermute(array, axis, [(i, (i + step) % peers) for i in range(peers)])
        out = lax.dynamic_update_slice_in_dim(out, moved, ((place - step) % peers) * rows, 0)
    return out


def spread_sum(value, axes):
    peers = lax.axis_size(axes)
    if peers > 64:
        return lax.psum(value, axes)
    return jnp.sum(spread_copy(jnp.full((8, 128), value), axes)[:, 0, 0])


def doc_layout(lengths_row, token_index):
    doc_ends = jnp.cumsum(lengths_row)
    passed = doc_ends[None, :] <= token_index[:, None]
    doc_start = jnp.max(jnp.where(passed, doc_ends[None, :], 0), axis=1)
    doc_id = jnp.sum(passed.astype(jnp.int32), axis=1)
    return (doc_id, (token_index - doc_start).astype(jnp.float32))


def rope_tables(position, rope_num, rope_den, head_dim):
    expo = jnp.arange(head_dim // 2, dtype=jnp.float32) * (2.0 / head_dim)
    freq = (
        jnp.exp(-math.log(ROPE_BASE) * expo)
        * rope_den.astype(jnp.float32)
        / rope_num.astype(jnp.float32)
    )
    angle = position[:, None] * freq[None, :]
    cosine = jnp.concatenate([jnp.cos(angle), jnp.cos(angle)], axis=1)
    sine = jnp.concatenate([jnp.sin(angle), jnp.sin(angle)], axis=1)
    return (cosine[:, None, :], sine[:, None, :])


def rotate(vectors, cosine, sine):
    half = vectors.shape[-1] // 2
    turned = jnp.concatenate([-vectors[..., half:], vectors[..., :half]], axis=-1)
    return vectors * cosine + turned * sine


def unrotate(grads_in, cosine, sine):
    half = grads_in.shape[-1] // 2
    scaled = grads_in * sine
    turned = jnp.concatenate([scaled[..., half:], -scaled[..., :half]], axis=-1)
    return grads_in * cosine + turned


def adam_update(param, first_moment_state, second_moment_state, weight_gradient, grad_total):
    clip_factor = jnp.minimum(jnp.float32(1.0), CLIP_NORM / jnp.sqrt(grad_total))
    clipped = weight_gradient * clip_factor
    new_first = BETA_ONE * first_moment_state + (1.0 - BETA_ONE) * clipped
    new_second = BETA_TWO * second_moment_state + (1.0 - BETA_TWO) * clipped * clipped
    step_size = new_first / FIRST_FIX / (jnp.sqrt(new_second / SECOND_FIX) + ADAM_EPS)
    new_param = param - LEARN_RATE * (step_size + DECAY_RATE * param)
    return (new_param, new_first, new_second)


def local(
    queries,
    keys,
    values,
    output_cotangent,
    features,
    doc_lengths,
    rope_num,
    rope_den,
    param,
    first_moment_state,
    second_moment_state,
):
    tok_rows = queries.shape[1]
    head_count = queries.shape[2]
    head_dim = queries.shape[3]
    kv_count = keys.shape[2]
    group_size = head_count // kv_count
    n_ctx = lax.axis_size("ctx")
    place = lax.axis_index("ctx")
    seq_len = tok_rows * n_ctx
    doc_most = seq_len // 32
    reach = (doc_most + tok_rows - 2) // tok_rows
    scale = head_dim ** (-0.5)
    lengths_row = doc_lengths[0]
    own_index = place * tok_rows + jnp.arange(tok_rows, dtype=jnp.int32)
    own_doc, position = doc_layout(lengths_row, own_index)
    cosine, sine = rope_tables(position, rope_num, rope_den, head_dim)
    rotated_query_rows = rotate(queries[0].astype(jnp.float32), cosine, sine).astype(jnp.bfloat16)
    rotated_query_rows = rotated_query_rows.reshape(tok_rows, kv_count, group_size, head_dim)
    rotated_key_rows = rotate(keys[0].astype(jnp.float32), cosine, sine).astype(jnp.bfloat16)
    grad_out = output_cotangent[0].reshape(tok_rows, kv_count, group_size, head_dim)
    kv_pair = jnp.stack([rotated_key_rows, values[0]])
    pairs = [kv_pair]
    offset = 1
    kv_pair = shifted(kv_pair, "ctx", 1)
    pairs.append(kv_pair)
    masks = []
    for offset in range(reach + 1):
        key_index = (place - offset) * tok_rows + jnp.arange(tok_rows, dtype=jnp.int32)
        key_doc = doc_layout(lengths_row, key_index)[0]
        valid = (
            (key_index[None, :] >= 0)
            & (key_index[None, :] <= own_index[:, None])
            & (key_doc[None, :] == own_doc[:, None])
        )
        masks.append(valid)
    score_list = []
    for pair_in, valid_in in zip(pairs, masks):
        raw = (
            jnp.einsum(
                "qhgd,khd->hgqk", rotated_query_rows, pair_in[0], preferred_element_type=jnp.float32
            )
            * scale
        )
        score_list.append(jnp.where(valid_in, raw, NEG_FILL))
    row_top = reduce(
        jnp.maximum, [jnp.max(scores, axis=-1, keepdims=True) for scores in score_list]
    )
    weight_list = [
        jnp.where(valid_in, jnp.exp(scores - row_top), 0.0)
        for scores, valid_in in zip(score_list, masks)
    ]
    row_total = reduce(
        jnp.add, [jnp.sum(weights, axis=-1, keepdims=True) for weights in weight_list]
    )
    prob_list = [weights / row_total for weights in weight_list]
    low_list = [probs.astype(jnp.bfloat16) for probs in prob_list]
    attn_out = reduce(
        jnp.add,
        [
            jnp.einsum("hgqk,khd->qhgd", probs_low, pair_in[1], preferred_element_type=jnp.float32)
            for probs_low, pair_in in zip(low_list, pairs)
        ],
    )
    delta = jnp.einsum("qhgd,qhgd->hgq", grad_out.astype(jnp.float32), attn_out)[..., None]
    value_terms = [
        jnp.einsum("hgqk,qhgd->khd", probs_low, grad_out, preferred_element_type=jnp.float32)
        for probs_low in low_list
    ]
    value_total = (
        shifted(value_terms[reach].astype(jnp.bfloat16), "ctx", -1).astype(jnp.float32)
        + value_terms[0]
    )
    grad_v = value_total.astype(jnp.bfloat16)
    query_terms = []
    key_terms = []
    for pair_in, probs, valid_in in zip(pairs, prob_list, masks):
        dprobs = jnp.einsum(
            "qhgd,khd->hgqk", grad_out, pair_in[1], preferred_element_type=jnp.float32
        )
        dscores = (probs * (dprobs - delta)).astype(jnp.bfloat16)
        q_part = (
            jnp.einsum("hgqk,khd->qhgd", dscores, pair_in[0], preferred_element_type=jnp.float32)
            * scale
        )
        k_part = (
            jnp.einsum(
                "hgqk,qhgd->khd", dscores, rotated_query_rows, preferred_element_type=jnp.float32
            )
            * scale
        )
        query_terms.append(q_part)
        key_terms.append(k_part)
    query_grad = reduce(jnp.add, query_terms)
    key_total = (
        shifted(key_terms[reach].astype(jnp.bfloat16), "ctx", -1).astype(jnp.float32)
        + key_terms[0]
    )
    grad_q = unrotate(query_grad.reshape(tok_rows, head_count, head_dim), cosine, sine).astype(
        jnp.bfloat16
    )
    grad_k = unrotate(key_total, cosine, sine).astype(jnp.bfloat16)
    feats = features[0]
    width = feats.shape[1]
    value_flat = grad_v.reshape(tok_rows, kv_count * head_dim)
    own_rows = param.shape[0]
    n_dp = lax.axis_size("dp")
    piece_rows = own_rows // n_ctx
    spread = ("ctx", "dp")
    by_place = feats.reshape(tok_rows, n_dp, n_ctx, piece_rows).transpose(0, 2, 1, 3)
    feat_cols = lax.all_to_all(
        by_place.reshape(tok_rows, n_dp * n_ctx, piece_rows), spread, 1, 0, tiled=False
    )
    if n_dp * n_ctx <= 16:
        value_rows = ring_copy(value_flat, spread)
    else:
        value_rows = spread_copy(value_flat, spread)
    pieces = lax.dot_general(
        feat_cols.reshape(-1, piece_rows),
        value_rows.reshape(-1, kv_count * head_dim),
        (((0,), (0,)), ((), ())),
        preferred_element_type=jnp.float32,
    )
    weight_gradient = ring_copy(pieces, "ctx")
    norm_part = jnp.sum(pieces * pieces)
    everyone = ("ctx", "dp", "tp")
    grad_total = spread_sum(norm_part, everyone)
    new_param, new_first, new_second = adam_update(
        param, first_moment_state, second_moment_state, weight_gradient, grad_total
    )
    return (grad_q[None], grad_k[None], grad_v[None], new_param, new_first, new_second)


def solution(mesh):
    placed = (
        P("dp", "ctx", "tp", None),
        P("dp", "ctx", "tp", None),
        P("dp", "ctx", "tp", None),
        P("dp", "ctx", "tp", None),
        P("dp", "ctx", None),
        P("dp", None),
        P(),
        P(),
        P("dp", "tp"),
        P("dp", "tp"),
        P("dp", "tp"),
    )
    return jax.shard_map(
        local,
        mesh=mesh,
        in_specs=placed,
        out_specs=(
            P("dp", "ctx", "tp", None),
            P("dp", "ctx", "tp", None),
            P("dp", "ctx", "tp", None),
            P("dp", "tp"),
            P("dp", "tp"),
            P("dp", "tp"),
        ),
        check_vma=False,
    )
```

```python
from functools import reduce
import math

import jax
import jax.numpy as jnp
from jax import lax
from jax.sharding import PartitionSpec as P

ROPE_BASE = 500000.0
NEG_FILL = -1e30
CLIP_NORM = 1000.0
LEARN_RATE = 0.0001
DECAY_RATE = 0.1
BETA_ONE = 0.9
BETA_TWO = 0.95
ADAM_EPS = 1e-08
FIRST_FIX = 1.0 - 0.9**10
SECOND_FIX = 1.0 - 0.95**10


def shifted(array, axis, by):
    peers = lax.axis_size(axis)
    pairs = [(i, i + by) for i in range(peers) if 0 <= i + by < peers]
    return lax.ppermute(array, axis, pairs)


def spread_copy(array, axes):
    peers = lax.axis_size(axes)
    if peers * array.size * array.dtype.itemsize > (4 << 20):
        return lax.all_gather(array, axes, axis=0, tiled=False)
    stacked = jnp.broadcast_to(array[None], (peers,) + array.shape)
    return lax.all_to_all(stacked, axes, 0, 0, tiled=False)


def ring_copy(array, axis):
    peers = lax.axis_size(axis)
    place = lax.axis_index(axis)
    rows = array.shape[0]
    out = jnp.zeros((peers * rows,) + array.shape[1:], array.dtype)
    out = lax.dynamic_update_slice_in_dim(out, array, place * rows, 0)
    for step in range(1, peers):
        moved = lax.ppermute(array, axis, [(i, (i + step) % peers) for i in range(peers)])
        out = lax.dynamic_update_slice_in_dim(out, moved, ((place - step) % peers) * rows, 0)
    return out


def spread_sum(value, axes):
    peers = lax.axis_size(axes)
    if peers > 64:
        return lax.psum(value, axes)
    return jnp.sum(spread_copy(jnp.full((8, 128), value), axes)[:, 0, 0])


def doc_layout(lengths_row, token_index):
    doc_ends = jnp.cumsum(lengths_row)
    passed = doc_ends[None, :] <= token_index[:, None]
    doc_start = jnp.max(jnp.where(passed, doc_ends[None, :], 0), axis=1)
    doc_id = jnp.sum(passed.astype(jnp.int32), axis=1)
    return (doc_id, (token_index - doc_start).astype(jnp.float32))


def rope_tables(position, rope_num, rope_den, head_dim):
    expo = jnp.arange(head_dim // 2, dtype=jnp.float32) * (2.0 / head_dim)
    freq = (
        jnp.exp(-math.log(ROPE_BASE) * expo)
        * rope_den.astype(jnp.float32)
        / rope_num.astype(jnp.float32)
    )
    angle = position[:, None] * freq[None, :]
    cosine = jnp.concatenate([jnp.cos(angle), jnp.cos(angle)], axis=1)
    sine = jnp.concatenate([jnp.sin(angle), jnp.sin(angle)], axis=1)
    return (cosine[:, None, :], sine[:, None, :])


def rotate(vectors, cosine, sine):
    half = vectors.shape[-1] // 2
    turned = jnp.concatenate([-vectors[..., half:], vectors[..., :half]], axis=-1)
    return vectors * cosine + turned * sine


def rotate_low(vectors, cosine, sine):
    half = vectors.shape[-1] // 2
    eye = jnp.eye(half, dtype=jnp.bfloat16)
    zero = jnp.zeros((half, half), jnp.bfloat16)
    swap = jnp.concatenate(
        [jnp.concatenate([zero, eye], axis=1), jnp.concatenate([-eye, zero], axis=1)], axis=0
    )
    turned = jnp.einsum("...d,de->...e", vectors, swap, preferred_element_type=jnp.float32)
    return vectors.astype(jnp.float32) * cosine + turned * sine


def unrotate(grads_in, cosine, sine):
    half = grads_in.shape[-1] // 2
    scaled = grads_in * sine
    turned = jnp.concatenate([scaled[..., half:], -scaled[..., :half]], axis=-1)
    return grads_in * cosine + turned


def adam_update(param, first_moment_state, second_moment_state, weight_gradient, grad_total):
    clip_factor = jnp.minimum(jnp.float32(1.0), CLIP_NORM / jnp.sqrt(grad_total))
    clipped = weight_gradient * clip_factor
    new_first = BETA_ONE * first_moment_state + (1.0 - BETA_ONE) * clipped
    new_second = BETA_TWO * second_moment_state + (1.0 - BETA_TWO) * clipped * clipped
    step_size = new_first / FIRST_FIX / (jnp.sqrt(new_second / SECOND_FIX) + ADAM_EPS)
    new_param = param - LEARN_RATE * (step_size + DECAY_RATE * param)
    return (new_param, new_first, new_second)


def local(
    queries,
    keys,
    values,
    output_cotangent,
    features,
    doc_lengths,
    rope_num,
    rope_den,
    param,
    first_moment_state,
    second_moment_state,
):
    tok_rows = queries.shape[1]
    head_count = queries.shape[2]
    head_dim = queries.shape[3]
    kv_count = keys.shape[2]
    group_size = head_count // kv_count
    n_ctx = lax.axis_size("ctx")
    place = lax.axis_index("ctx")
    seq_len = tok_rows * n_ctx
    doc_most = seq_len // 32
    reach = (doc_most + tok_rows - 2) // tok_rows
    scale = head_dim ** (-0.5)
    lengths_row = doc_lengths[0]
    own_index = place * tok_rows + jnp.arange(tok_rows, dtype=jnp.int32)
    own_doc, position = doc_layout(lengths_row, own_index)
    cosine, sine = rope_tables(position, rope_num, rope_den, head_dim)
    rotated_query_rows = rotate_low(queries[0], cosine, sine).astype(jnp.bfloat16)
    rotated_query_rows = rotated_query_rows.reshape(tok_rows, kv_count, group_size, head_dim)
    rotated_key_rows = rotate_low(keys[0], cosine, sine).astype(jnp.bfloat16)
    grad_out = output_cotangent[0].reshape(tok_rows, kv_count, group_size, head_dim)
    kv_pair = jnp.stack([rotated_key_rows, values[0]])
    pairs = [kv_pair]
    offset = 1
    kv_pair = shifted(kv_pair, "ctx", 1)
    pairs.append(kv_pair)
    masks = []
    for offset in range(reach + 1):
        key_index = (place - offset) * tok_rows + jnp.arange(tok_rows, dtype=jnp.int32)
        key_doc = doc_layout(lengths_row, key_index)[0]
        valid = (
            (key_index[None, :] >= 0)
            & (key_index[None, :] <= own_index[:, None])
            & (key_doc[None, :] == own_doc[:, None])
        )
        masks.append(valid)
    score_list = []
    for pair_in, valid_in in zip(pairs, masks):
        raw = (
            jnp.einsum(
                "qhgd,khd->hgqk", rotated_query_rows, pair_in[0], preferred_element_type=jnp.float32
            )
            * scale
        )
        score_list.append(jnp.where(valid_in, raw, NEG_FILL))
    row_top = reduce(
        jnp.maximum, [jnp.max(scores, axis=-1, keepdims=True) for scores in score_list]
    )
    weight_list = [
        jnp.where(valid_in, jnp.exp(scores - row_top), 0.0)
        for scores, valid_in in zip(score_list, masks)
    ]
    row_total = reduce(
        jnp.add, [jnp.sum(weights, axis=-1, keepdims=True) for weights in weight_list]
    )
    prob_list = [weights / row_total for weights in weight_list]
    low_list = [probs.astype(jnp.bfloat16) for probs in prob_list]
    attn_out = reduce(
        jnp.add,
        [
            jnp.einsum("hgqk,khd->qhgd", probs_low, pair_in[1], preferred_element_type=jnp.float32)
            for probs_low, pair_in in zip(low_list, pairs)
        ],
    )
    delta = jnp.einsum("qhgd,qhgd->hgq", grad_out.astype(jnp.float32), attn_out)[..., None]
    query_terms = []
    key_terms = []
    for pair_in, probs, probs_low, valid_in in zip(pairs, prob_list, low_list, masks):
        dprobs = jnp.einsum(
            "qhgd,khd->hgqk", grad_out, pair_in[1], preferred_element_type=jnp.float32
        )
        dscores = (probs * (dprobs - delta)).astype(jnp.bfloat16)
        q_part = (
            jnp.einsum("hgqk,khd->qhgd", dscores, pair_in[0], preferred_element_type=jnp.float32)
            * scale
        )
        k_part = (
            jnp.einsum(
                "hgqk,qhgd->khd", dscores, rotated_query_rows, preferred_element_type=jnp.float32
            )
            * scale
        )
        v_part = jnp.einsum(
            "hgqk,qhgd->khd", probs_low, grad_out, preferred_element_type=jnp.float32
        )
        q_part, kv_part = (q_part, jnp.stack([k_part, v_part]))
        query_terms.append(q_part)
        key_terms.append(kv_part)
    query_grad = reduce(jnp.add, query_terms)
    key_total = key_terms[reach]
    offset = 0
    key_total = (
        shifted(key_total.astype(jnp.bfloat16), "ctx", -1).astype(key_total.dtype)
        + key_terms[offset]
    )
    grad_q = unrotate(query_grad.reshape(tok_rows, head_count, head_dim), cosine, sine).astype(
        jnp.bfloat16
    )
    grad_k = unrotate(key_total[0], cosine, sine).astype(jnp.bfloat16)
    grad_v = key_total[1].astype(jnp.bfloat16)
    feats = features[0]
    width = feats.shape[1]
    value_flat = grad_v.reshape(tok_rows, kv_count * head_dim)
    own_rows = param.shape[0]
    n_dp = lax.axis_size("dp")
    piece_rows = own_rows // n_ctx
    spread = ("dp", "ctx")
    feat_cols = lax.all_to_all(
        feats.reshape(tok_rows, n_dp * n_ctx, piece_rows), spread, 1, 0, tiled=False
    )
    value_rows = spread_copy(value_flat, spread)
    pieces = lax.dot_general(
        feat_cols.reshape(-1, piece_rows),
        value_rows.reshape(-1, kv_count * head_dim),
        (((0,), (0,)), ((), ())),
        preferred_element_type=jnp.float32,
    )
    weight_gradient = ring_copy(pieces, "ctx")
    norm_part = jnp.sum(pieces * pieces)
    everyone = ("ctx", "dp", "tp")
    grad_total = spread_sum(norm_part, everyone)
    new_param, new_first, new_second = adam_update(
        param, first_moment_state, second_moment_state, weight_gradient, grad_total
    )
    return (grad_q[None], grad_k[None], grad_v[None], new_param, new_first, new_second)


def solution(mesh):
    placed = (
        P("dp", "ctx", "tp", None),
        P("dp", "ctx", "tp", None),
        P("dp", "ctx", "tp", None),
        P("dp", "ctx", "tp", None),
        P("dp", "ctx", None),
        P("dp", None),
        P(),
        P(),
        P("dp", "tp"),
        P("dp", "tp"),
        P("dp", "tp"),
    )
    return jax.shard_map(
        local,
        mesh=mesh,
        in_specs=placed,
        out_specs=(
            P("dp", "ctx", "tp", None),
            P("dp", "ctx", "tp", None),
            P("dp", "ctx", "tp", None),
            P("dp", "tp"),
            P("dp", "tp"),
            P("dp", "tp"),
        ),
        check_vma=False,
    )
```

```python
from functools import reduce
import math

import jax
import jax.numpy as jnp
from jax import lax
from jax.sharding import PartitionSpec as P


ROPE_BASE = 500000.0
NEG_FILL = -1e30
CLIP_NORM = 1000.0
LEARN_RATE = 0.0001
DECAY_RATE = 0.1
BETA_ONE = 0.9
BETA_TWO = 0.95
ADAM_EPS = 1e-08
FIRST_FIX = 1.0 - 0.9**10
SECOND_FIX = 1.0 - 0.95**10


def shifted(array, axis, by):
    peers = lax.axis_size(axis)
    pairs = [(i, i + by) for i in range(peers) if 0 <= i + by < peers]
    return lax.ppermute(array, axis, pairs)


def spread_copy(array, axes):
    peers = lax.axis_size(axes)
    if peers * array.size * array.dtype.itemsize > (4 << 20):
        return lax.all_gather(array, axes, axis=0, tiled=False)
    stacked = jnp.broadcast_to(array[None], (peers,) + array.shape)
    return lax.all_to_all(stacked, axes, 0, 0, tiled=False)


def ring_copy(array, axis):
    peers = lax.axis_size(axis)
    place = lax.axis_index(axis)
    rows = array.shape[0]
    out = jnp.zeros((peers * rows,) + array.shape[1:], array.dtype)
    out = lax.dynamic_update_slice_in_dim(out, array, place * rows, 0)
    for step in range(1, peers):
        moved = lax.ppermute(array, axis, [(i, (i + step) % peers) for i in range(peers)])
        out = lax.dynamic_update_slice_in_dim(out, moved, ((place - step) % peers) * rows, 0)
    return out


def spread_sum(value, axes):
    peers = lax.axis_size(axes)
    if peers > 64:
        return lax.psum(value, axes)
    return jnp.sum(spread_copy(jnp.full((8, 128), value), axes)[:, 0, 0])


def doc_layout(lengths_row, token_index):
    doc_ends = jnp.cumsum(lengths_row)
    passed = doc_ends[None, :] <= token_index[:, None]
    doc_start = jnp.max(jnp.where(passed, doc_ends[None, :], 0), axis=1)
    doc_id = jnp.sum(passed.astype(jnp.int32), axis=1)
    return (doc_id, (token_index - doc_start).astype(jnp.float32))


def rope_tables(position, rope_num, rope_den, head_dim):
    expo = jnp.arange(head_dim // 2, dtype=jnp.float32) * (2.0 / head_dim)
    freq = (
        jnp.exp(-math.log(ROPE_BASE) * expo)
        * rope_den.astype(jnp.float32)
        / rope_num.astype(jnp.float32)
    )
    angle = position[:, None] * freq[None, :]
    cosine = jnp.concatenate([jnp.cos(angle), jnp.cos(angle)], axis=1)
    sine = jnp.concatenate([jnp.sin(angle), jnp.sin(angle)], axis=1)
    return (cosine[:, None, :], sine[:, None, :])


def rotate_low(vectors, cosine, sine):
    half = vectors.shape[-1] // 2
    eye = jnp.eye(half, dtype=jnp.bfloat16)
    zero = jnp.zeros((half, half), jnp.bfloat16)
    swap = jnp.concatenate(
        [jnp.concatenate([zero, eye], axis=1), jnp.concatenate([-eye, zero], axis=1)], axis=0
    )
    turned = jnp.einsum("...d,de->...e", vectors, swap, preferred_element_type=jnp.float32)
    return vectors.astype(jnp.float32) * cosine + turned * sine


def unrotate(grads_in, cosine, sine):
    half = grads_in.shape[-1] // 2
    scaled = grads_in * sine
    turned = jnp.concatenate([scaled[..., half:], -scaled[..., :half]], axis=-1)
    return grads_in * cosine + turned


def adam_update(param, first_moment_state, second_moment_state, weight_gradient, grad_total):
    clip_factor = jnp.minimum(jnp.float32(1.0), CLIP_NORM / jnp.sqrt(grad_total))
    clipped = weight_gradient * clip_factor
    new_first = BETA_ONE * first_moment_state + (1.0 - BETA_ONE) * clipped
    new_second = BETA_TWO * second_moment_state + (1.0 - BETA_TWO) * clipped * clipped
    step_size = new_first / FIRST_FIX / (jnp.sqrt(new_second / SECOND_FIX) + ADAM_EPS)
    new_param = param - LEARN_RATE * (step_size + DECAY_RATE * param)
    return (new_param, new_first, new_second)


def local_body(
    queries,
    keys,
    values,
    output_cotangent,
    features,
    doc_lengths,
    rope_num,
    rope_den,
    param,
    first_moment_state,
    second_moment_state,
):
    tok_rows = queries.shape[1]
    head_count = queries.shape[2]
    head_dim = queries.shape[3]
    kv_count = keys.shape[2]
    group_size = head_count // kv_count
    n_ctx = lax.axis_size("ctx")
    place = lax.axis_index("ctx")
    seq_len = tok_rows * n_ctx
    doc_most = seq_len // 32
    reach = (doc_most + tok_rows - 2) // tok_rows
    scale = head_dim ** (-0.5)
    lengths_row = doc_lengths[0]
    own_index = place * tok_rows + jnp.arange(tok_rows, dtype=jnp.int32)
    own_doc, position = doc_layout(lengths_row, own_index)
    cosine, sine = rope_tables(position, rope_num, rope_den, head_dim)
    rotated_query_rows = rotate_low(queries[0], cosine, sine).astype(jnp.bfloat16)
    rotated_query_rows = rotated_query_rows.reshape(tok_rows, kv_count, group_size, head_dim)
    rotated_key_rows = rotate_low(keys[0], cosine, sine).astype(jnp.bfloat16)
    grad_out = output_cotangent[0].reshape(tok_rows, kv_count, group_size, head_dim)
    kv_pair = jnp.stack([rotated_key_rows, values[0]])
    pairs = [kv_pair]
    offset = 1
    kv_pair = shifted(kv_pair, "ctx", 1)
    pairs.append(kv_pair)
    masks = []
    for offset in range(reach + 1):
        key_index = (place - offset) * tok_rows + jnp.arange(tok_rows, dtype=jnp.int32)
        key_doc = doc_layout(lengths_row, key_index)[0]
        valid = (
            (key_index[None, :] >= 0)
            & (key_index[None, :] <= own_index[:, None])
            & (key_doc[None, :] == own_doc[:, None])
        )
        masks.append(valid)
    score_list = []
    for pair_in, valid_in in zip(pairs, masks):
        raw = (
            jnp.einsum(
                "qhgd,khd->hgqk", rotated_query_rows, pair_in[0], preferred_element_type=jnp.float32
            )
            * scale
        )
        score_list.append(jnp.where(valid_in, raw, NEG_FILL))
    row_top = reduce(
        jnp.maximum, [jnp.max(scores, axis=-1, keepdims=True) for scores in score_list]
    )
    weight_list = [
        jnp.where(valid_in, jnp.exp(scores - row_top), 0.0)
        for scores, valid_in in zip(score_list, masks)
    ]
    row_total = reduce(
        jnp.add, [jnp.sum(weights, axis=-1, keepdims=True) for weights in weight_list]
    )
    prob_list = [weights / row_total for weights in weight_list]
    low_list = [probs.astype(jnp.bfloat16) for probs in prob_list]
    attn_out = reduce(
        jnp.add,
        [
            jnp.einsum("hgqk,khd->qhgd", probs_low, pair_in[1], preferred_element_type=jnp.float32)
            for probs_low, pair_in in zip(low_list, pairs)
        ],
    )
    delta = jnp.einsum("qhgd,qhgd->hgq", grad_out.astype(jnp.float32), attn_out)[..., None]
    query_terms = []
    key_terms = []
    for pair_in, probs, probs_low, valid_in in zip(pairs, prob_list, low_list, masks):
        dprobs = jnp.einsum(
            "qhgd,khd->hgqk", grad_out, pair_in[1], preferred_element_type=jnp.float32
        )
        dscores = (probs * (dprobs - delta)).astype(jnp.bfloat16)
        q_part = (
            jnp.einsum("hgqk,khd->qhgd", dscores, pair_in[0], preferred_element_type=jnp.float32)
            * scale
        )
        k_part = (
            jnp.einsum(
                "hgqk,qhgd->khd", dscores, rotated_query_rows, preferred_element_type=jnp.float32
            )
            * scale
        )
        v_part = jnp.einsum(
            "hgqk,qhgd->khd", probs_low, grad_out, preferred_element_type=jnp.float32
        )
        q_part, kv_part = (q_part, jnp.stack([k_part, v_part]))
        query_terms.append(q_part)
        key_terms.append(kv_part)
    query_grad = reduce(jnp.add, query_terms)
    key_total = key_terms[reach]
    offset = 0
    key_total = (
        shifted(key_total.astype(jnp.bfloat16), "ctx", -1).astype(key_total.dtype)
        + key_terms[offset]
    )
    grad_q = unrotate(query_grad.reshape(tok_rows, head_count, head_dim), cosine, sine).astype(
        jnp.bfloat16
    )
    grad_k = unrotate(key_total[0], cosine, sine).astype(jnp.bfloat16)
    grad_v = key_total[1].astype(jnp.bfloat16)
    feats = features[0]
    value_flat = grad_v.reshape(tok_rows, kv_count * head_dim)
    own_rows = param.shape[0]
    n_dp = lax.axis_size("dp")
    piece_rows = own_rows // n_ctx
    spread = ("dp", "ctx")
    feat_cols = lax.all_to_all(
        feats.reshape(tok_rows, n_dp * n_ctx, piece_rows), spread, 1, 0, tiled=False
    )
    value_rows = spread_copy(value_flat, spread)
    pieces = lax.dot_general(
        feat_cols.reshape(-1, piece_rows),
        value_rows.reshape(-1, kv_count * head_dim),
        (((0,), (0,)), ((), ())),
        preferred_element_type=jnp.float32,
    )
    weight_gradient = ring_copy(pieces, "ctx")
    norm_part = jnp.sum(pieces * pieces)
    everyone = ("ctx", "dp", "tp")
    grad_total = spread_sum(norm_part, everyone)
    new_param, new_first, new_second = adam_update(
        param, first_moment_state, second_moment_state, weight_gradient, grad_total
    )
    return (grad_q[None], grad_k[None], grad_v[None], new_param, new_first, new_second)


def solution(mesh):
    placed = (
        P("dp", "ctx", "tp", None),
        P("dp", "ctx", "tp", None),
        P("dp", "ctx", "tp", None),
        P("dp", "ctx", "tp", None),
        P("dp", "ctx", None),
        P("dp", None),
        P(),
        P(),
        P("dp", "tp"),
        P("dp", "tp"),
        P("dp", "tp"),
    )
    return jax.shard_map(
        local_body,
        mesh=mesh,
        in_specs=placed,
        out_specs=(
            P("dp", "ctx", "tp", None),
            P("dp", "ctx", "tp", None),
            P("dp", "ctx", "tp", None),
            P("dp", "tp"),
            P("dp", "tp"),
            P("dp", "tp"),
        ),
        check_vma=False,
    )
```

```python
from functools import reduce
import math

import jax
import jax.numpy as jnp
from jax import lax
from jax.sharding import PartitionSpec as P


ROPE_BASE = 500000.0
NEG_FILL = -1e30
CLIP_NORM = 1000.0
LEARN_RATE = 0.0001
DECAY_RATE = 0.1
BETA_ONE = 0.9
BETA_TWO = 0.95
ADAM_EPS = 1e-08
FIRST_FIX = 1.0 - 0.9**10
SECOND_FIX = 1.0 - 0.95**10


def shifted(array, axis, by):
    peers = lax.axis_size(axis)
    pairs = [(i, i + by) for i in range(peers) if 0 <= i + by < peers]
    return lax.ppermute(array, axis, pairs)


def spread_copy(array, axes):
    peers = lax.axis_size(axes)
    if peers * array.size * array.dtype.itemsize > (4 << 20):
        return lax.all_gather(array, axes, axis=0, tiled=False)
    stacked = jnp.broadcast_to(array[None], (peers,) + array.shape)
    return lax.all_to_all(stacked, axes, 0, 0, tiled=False)


def ring_copy(array, axis):
    peers = lax.axis_size(axis)
    place = lax.axis_index(axis)
    rows = array.shape[0]
    out = jnp.zeros((peers * rows,) + array.shape[1:], array.dtype)
    out = lax.dynamic_update_slice_in_dim(out, array, place * rows, 0)
    for step in range(1, peers):
        moved = lax.ppermute(array, axis, [(i, (i + step) % peers) for i in range(peers)])
        out = lax.dynamic_update_slice_in_dim(out, moved, ((place - step) % peers) * rows, 0)
    return out


def doubling_copy(array, axis):
    peers = lax.axis_size(axis)
    if peers & (peers - 1):
        return ring_copy(array, axis)
    place = lax.axis_index(axis)
    gathered = array
    span = 1
    while span < peers:
        other = lax.ppermute(gathered, axis, [(i, i ^ span) for i in range(peers)])
        low_half = (place & span) == 0
        gathered = jnp.where(
            low_half,
            jnp.concatenate([gathered, other], axis=0),
            jnp.concatenate([other, gathered], axis=0),
        )
        span *= 2
    return gathered


def spread_sum(value, axes):
    peers = lax.axis_size(axes)
    if peers > 64:
        return lax.psum(value, axes)
    return jnp.sum(spread_copy(jnp.full((8, 128), value), axes)[:, 0, 0])


def doc_layout(lengths_row, token_index):
    doc_ends = jnp.cumsum(lengths_row)
    passed = doc_ends[None, :] <= token_index[:, None]
    doc_start = jnp.max(jnp.where(passed, doc_ends[None, :], 0), axis=1)
    doc_id = jnp.sum(passed.astype(jnp.int32), axis=1)
    return (doc_id, (token_index - doc_start).astype(jnp.float32))


def rope_tables(position, rope_num, rope_den, head_dim):
    expo = jnp.arange(head_dim // 2, dtype=jnp.float32) * (2.0 / head_dim)
    freq = (
        jnp.exp(-math.log(ROPE_BASE) * expo)
        * rope_den.astype(jnp.float32)
        / rope_num.astype(jnp.float32)
    )
    angle = position[:, None] * freq[None, :]
    cosine = jnp.concatenate([jnp.cos(angle), jnp.cos(angle)], axis=1)
    sine = jnp.concatenate([jnp.sin(angle), jnp.sin(angle)], axis=1)
    return (cosine[:, None, :], sine[:, None, :])


def rotate_low(vectors, cosine, sine):
    half = vectors.shape[-1] // 2
    eye = jnp.eye(half, dtype=jnp.bfloat16)
    zero = jnp.zeros((half, half), jnp.bfloat16)
    swap = jnp.concatenate(
        [jnp.concatenate([zero, eye], axis=1), jnp.concatenate([-eye, zero], axis=1)], axis=0
    )
    turned = jnp.einsum("...d,de->...e", vectors, swap, preferred_element_type=jnp.float32)
    return vectors.astype(jnp.float32) * cosine + turned * sine


def unrotate(grads_in, cosine, sine):
    half = grads_in.shape[-1] // 2
    scaled = grads_in * sine
    turned = jnp.concatenate([scaled[..., half:], -scaled[..., :half]], axis=-1)
    return grads_in * cosine + turned


def adam_update(param, first_moment_state, second_moment_state, weight_gradient, grad_total):
    clip_factor = jnp.minimum(jnp.float32(1.0), CLIP_NORM / jnp.sqrt(grad_total))
    clipped = weight_gradient * clip_factor
    new_first = BETA_ONE * first_moment_state + (1.0 - BETA_ONE) * clipped
    new_second = BETA_TWO * second_moment_state + (1.0 - BETA_TWO) * clipped * clipped
    step_size = new_first / FIRST_FIX / (jnp.sqrt(new_second / SECOND_FIX) + ADAM_EPS)
    new_param = param - LEARN_RATE * (step_size + DECAY_RATE * param)
    return (new_param, new_first, new_second)


def local_body(
    queries,
    keys,
    values,
    output_cotangent,
    features,
    doc_lengths,
    rope_num,
    rope_den,
    param,
    first_moment_state,
    second_moment_state,
):
    tok_rows = queries.shape[1]
    head_count = queries.shape[2]
    head_dim = queries.shape[3]
    kv_count = keys.shape[2]
    group_size = head_count // kv_count
    n_ctx = lax.axis_size("ctx")
    place = lax.axis_index("ctx")
    seq_len = tok_rows * n_ctx
    doc_most = seq_len // 32
    reach = (doc_most + tok_rows - 2) // tok_rows
    scale = head_dim ** (-0.5)
    lengths_row = doc_lengths[0]
    own_index = place * tok_rows + jnp.arange(tok_rows, dtype=jnp.int32)
    own_doc, position = doc_layout(lengths_row, own_index)
    cosine, sine = rope_tables(position, rope_num, rope_den, head_dim)
    rotated_query_rows = rotate_low(queries[0], cosine, sine).astype(jnp.bfloat16)
    rotated_query_rows = rotated_query_rows.reshape(tok_rows, kv_count, group_size, head_dim)
    rotated_key_rows = rotate_low(keys[0], cosine, sine).astype(jnp.bfloat16)
    grad_out = output_cotangent[0].reshape(tok_rows, kv_count, group_size, head_dim)
    kv_pair = jnp.stack([rotated_key_rows, values[0]])
    pairs = [kv_pair]
    offset = 1
    kv_pair = shifted(kv_pair, "ctx", 1)
    pairs.append(kv_pair)
    masks = []
    for offset in range(reach + 1):
        key_index = (place - offset) * tok_rows + jnp.arange(tok_rows, dtype=jnp.int32)
        key_doc = doc_layout(lengths_row, key_index)[0]
        valid = (
            (key_index[None, :] >= 0)
            & (key_index[None, :] <= own_index[:, None])
            & (key_doc[None, :] == own_doc[:, None])
        )
        masks.append(valid)
    score_list = []
    for pair_in, valid_in in zip(pairs, masks):
        raw = (
            jnp.einsum(
                "qhgd,khd->hgqk", rotated_query_rows, pair_in[0], preferred_element_type=jnp.float32
            )
            * scale
        )
        score_list.append(jnp.where(valid_in, raw, NEG_FILL))
    row_top = reduce(
        jnp.maximum, [jnp.max(scores, axis=-1, keepdims=True) for scores in score_list]
    )
    weight_list = [
        jnp.where(valid_in, jnp.exp(scores - row_top), 0.0)
        for scores, valid_in in zip(score_list, masks)
    ]
    row_total = reduce(
        jnp.add, [jnp.sum(weights, axis=-1, keepdims=True) for weights in weight_list]
    )
    prob_list = [weights / row_total for weights in weight_list]
    low_list = [probs.astype(jnp.bfloat16) for probs in prob_list]
    attn_out = reduce(
        jnp.add,
        [
            jnp.einsum("hgqk,khd->qhgd", probs_low, pair_in[1], preferred_element_type=jnp.float32)
            for probs_low, pair_in in zip(low_list, pairs)
        ],
    )
    delta = jnp.einsum("qhgd,qhgd->hgq", grad_out.astype(jnp.float32), attn_out)[..., None]
    value_terms = [
        jnp.einsum("hgqk,qhgd->khd", probs_low, grad_out, preferred_element_type=jnp.float32)
        for probs_low in low_list
    ]
    value_total = (
        shifted(value_terms[reach].astype(jnp.bfloat16), "ctx", -1).astype(jnp.float32)
        + value_terms[0]
    )
    grad_v = value_total.astype(jnp.bfloat16)
    query_terms = []
    key_terms = []
    for pair_in, probs, valid_in in zip(pairs, prob_list, masks):
        dprobs = jnp.einsum(
            "qhgd,khd->hgqk", grad_out, pair_in[1], preferred_element_type=jnp.float32
        )
        dscores = (probs * (dprobs - delta)).astype(jnp.bfloat16)
        q_part = (
            jnp.einsum("hgqk,khd->qhgd", dscores, pair_in[0], preferred_element_type=jnp.float32)
            * scale
        )
        k_part = (
            jnp.einsum(
                "hgqk,qhgd->khd", dscores, rotated_query_rows, preferred_element_type=jnp.float32
            )
            * scale
        )
        query_terms.append(q_part)
        key_terms.append(k_part)
    query_grad = reduce(jnp.add, query_terms)
    key_total = (
        shifted(key_terms[reach].astype(jnp.bfloat16), "ctx", -1).astype(jnp.float32)
        + key_terms[0]
    )
    grad_q = unrotate(query_grad.reshape(tok_rows, head_count, head_dim), cosine, sine).astype(
        jnp.bfloat16
    )
    grad_k = unrotate(key_total, cosine, sine).astype(jnp.bfloat16)
    feats = features[0]
    value_flat = grad_v.reshape(tok_rows, kv_count * head_dim)
    own_rows = param.shape[0]
    n_dp = lax.axis_size("dp")
    piece_rows = own_rows // n_ctx
    spread = ("dp", "ctx")
    feat_cols = lax.all_to_all(
        feats.reshape(tok_rows, n_dp * n_ctx, piece_rows), spread, 1, 0, tiled=False
    )
    value_rows = spread_copy(value_flat, spread)
    pieces = lax.dot_general(
        feat_cols.reshape(-1, piece_rows),
        value_rows.reshape(-1, kv_count * head_dim),
        (((0,), (0,)), ((), ())),
        preferred_element_type=jnp.float32,
    )
    weight_gradient = doubling_copy(pieces, "ctx")
    norm_part = jnp.sum(pieces * pieces)
    everyone = ("ctx", "dp", "tp")
    grad_total = spread_sum(norm_part, everyone)
    new_param, new_first, new_second = adam_update(
        param, first_moment_state, second_moment_state, weight_gradient, grad_total
    )
    return (grad_q[None], grad_k[None], grad_v[None], new_param, new_first, new_second)


def solution(mesh):
    placed = (
        P("dp", "ctx", "tp", None),
        P("dp", "ctx", "tp", None),
        P("dp", "ctx", "tp", None),
        P("dp", "ctx", "tp", None),
        P("dp", "ctx", None),
        P("dp", None),
        P(),
        P(),
        P("dp", "tp"),
        P("dp", "tp"),
        P("dp", "tp"),
    )
    return jax.shard_map(
        local_body,
        mesh=mesh,
        in_specs=placed,
        out_specs=(
            P("dp", "ctx", "tp", None),
            P("dp", "ctx", "tp", None),
            P("dp", "ctx", "tp", None),
            P("dp", "tp"),
            P("dp", "tp"),
            P("dp", "tp"),
        ),
        check_vma=False,
    )
```

```python
from functools import reduce
import math

import jax
import jax.numpy as jnp
from jax import lax
from jax.sharding import PartitionSpec as P


ROPE_BASE = 500000.0
NEG_FILL = -1e30
CLIP_NORM = 1000.0
LEARN_RATE = 0.0001
DECAY_RATE = 0.1
BETA_ONE = 0.9
BETA_TWO = 0.95
ADAM_EPS = 1e-08
FIRST_FIX = 1.0 - 0.9**10
SECOND_FIX = 1.0 - 0.95**10


def shifted(array, axis, by):
    peers = lax.axis_size(axis)
    pairs = [(i, i + by) for i in range(peers) if 0 <= i + by < peers]
    return lax.ppermute(array, axis, pairs)


def spread_copy(array, axes):
    peers = lax.axis_size(axes)
    if peers * array.size * array.dtype.itemsize > (4 << 20):
        return lax.all_gather(array, axes, axis=0, tiled=False)
    stacked = jnp.broadcast_to(array[None], (peers,) + array.shape)
    return lax.all_to_all(stacked, axes, 0, 0, tiled=False)


def ring_copy(array, axis):
    peers = lax.axis_size(axis)
    place = lax.axis_index(axis)
    rows = array.shape[0]
    out = jnp.zeros((peers * rows,) + array.shape[1:], array.dtype)
    out = lax.dynamic_update_slice_in_dim(out, array, place * rows, 0)
    for step in range(1, peers):
        moved = lax.ppermute(array, axis, [(i, (i + step) % peers) for i in range(peers)])
        out = lax.dynamic_update_slice_in_dim(out, moved, ((place - step) % peers) * rows, 0)
    return out


def spread_sum(value, axes):
    peers = lax.axis_size(axes)
    if peers > 64:
        return lax.psum(value, axes)
    return jnp.sum(spread_copy(jnp.full((1, 128), value), axes)[:, 0, 0])


def doc_layout(lengths_row, token_index):
    doc_ends = jnp.cumsum(lengths_row)
    passed = doc_ends[None, :] <= token_index[:, None]
    doc_start = jnp.max(jnp.where(passed, doc_ends[None, :], 0), axis=1)
    doc_id = jnp.sum(passed.astype(jnp.int32), axis=1)
    return (doc_id, (token_index - doc_start).astype(jnp.float32))


def rope_tables(position, rope_num, rope_den, head_dim):
    expo = jnp.arange(head_dim // 2, dtype=jnp.float32) * (2.0 / head_dim)
    freq = (
        jnp.exp(-math.log(ROPE_BASE) * expo)
        * rope_den.astype(jnp.float32)
        / rope_num.astype(jnp.float32)
    )
    angle = position[:, None] * freq[None, :]
    cosine = jnp.concatenate([jnp.cos(angle), jnp.cos(angle)], axis=1)
    sine = jnp.concatenate([jnp.sin(angle), jnp.sin(angle)], axis=1)
    return (cosine[:, None, :], sine[:, None, :])


def rotate_low(vectors, cosine, sine):
    half = vectors.shape[-1] // 2
    eye = jnp.eye(half, dtype=jnp.bfloat16)
    zero = jnp.zeros((half, half), jnp.bfloat16)
    swap = jnp.concatenate(
        [jnp.concatenate([zero, eye], axis=1), jnp.concatenate([-eye, zero], axis=1)], axis=0
    )
    turned = jnp.einsum("...d,de->...e", vectors, swap, preferred_element_type=jnp.float32)
    return vectors.astype(jnp.float32) * cosine + turned * sine


def unrotate(grads_in, cosine, sine):
    half = grads_in.shape[-1] // 2
    scaled = grads_in * sine
    turned = jnp.concatenate([scaled[..., half:], -scaled[..., :half]], axis=-1)
    return grads_in * cosine + turned


def adam_update(param, first_moment_state, second_moment_state, weight_gradient, grad_total):
    clip_factor = jnp.minimum(jnp.float32(1.0), CLIP_NORM / jnp.sqrt(grad_total))
    clipped = weight_gradient * clip_factor
    new_first = BETA_ONE * first_moment_state + (1.0 - BETA_ONE) * clipped
    new_second = BETA_TWO * second_moment_state + (1.0 - BETA_TWO) * clipped * clipped
    step_size = new_first / FIRST_FIX / (jnp.sqrt(new_second / SECOND_FIX) + ADAM_EPS)
    new_param = param - LEARN_RATE * (step_size + DECAY_RATE * param)
    return (new_param, new_first, new_second)


def local_body(
    queries,
    keys,
    values,
    output_cotangent,
    features,
    doc_lengths,
    rope_num,
    rope_den,
    param,
    first_moment_state,
    second_moment_state,
):
    tok_rows = queries.shape[1]
    head_count = queries.shape[2]
    head_dim = queries.shape[3]
    kv_count = keys.shape[2]
    group_size = head_count // kv_count
    n_ctx = lax.axis_size("ctx")
    place = lax.axis_index("ctx")
    seq_len = tok_rows * n_ctx
    doc_most = seq_len // 32
    reach = (doc_most + tok_rows - 2) // tok_rows
    scale = head_dim ** (-0.5)
    lengths_row = doc_lengths[0]
    own_index = place * tok_rows + jnp.arange(tok_rows, dtype=jnp.int32)
    own_doc, position = doc_layout(lengths_row, own_index)
    cosine, sine = rope_tables(position, rope_num, rope_den, head_dim)
    rotated_query_rows = rotate_low(queries[0], cosine, sine).astype(jnp.bfloat16)
    rotated_query_rows = rotated_query_rows.reshape(tok_rows, kv_count, group_size, head_dim)
    rotated_key_rows = rotate_low(keys[0], cosine, sine).astype(jnp.bfloat16)
    grad_out = output_cotangent[0].reshape(tok_rows, kv_count, group_size, head_dim)
    kv_pair = jnp.stack([rotated_key_rows, values[0]])
    pairs = [kv_pair]
    offset = 1
    kv_pair = shifted(kv_pair, "ctx", 1)
    pairs.append(kv_pair)
    masks = []
    for offset in range(reach + 1):
        key_index = (place - offset) * tok_rows + jnp.arange(tok_rows, dtype=jnp.int32)
        key_doc = doc_layout(lengths_row, key_index)[0]
        valid = (
            (key_index[None, :] >= 0)
            & (key_index[None, :] <= own_index[:, None])
            & (key_doc[None, :] == own_doc[:, None])
        )
        masks.append(valid)
    score_list = []
    for pair_in, valid_in in zip(pairs, masks):
        raw = (
            jnp.einsum(
                "qhgd,khd->hgqk", rotated_query_rows, pair_in[0], preferred_element_type=jnp.float32
            )
            * scale
        )
        score_list.append(jnp.where(valid_in, raw, NEG_FILL))
    row_top = reduce(
        jnp.maximum, [jnp.max(scores, axis=-1, keepdims=True) for scores in score_list]
    )
    weight_list = [
        jnp.where(valid_in, jnp.exp(scores - row_top), 0.0)
        for scores, valid_in in zip(score_list, masks)
    ]
    row_total = reduce(
        jnp.add, [jnp.sum(weights, axis=-1, keepdims=True) for weights in weight_list]
    )
    prob_list = [weights / row_total for weights in weight_list]
    low_list = [probs.astype(jnp.bfloat16) for probs in prob_list]
    attn_out = reduce(
        jnp.add,
        [
            jnp.einsum("hgqk,khd->qhgd", probs_low, pair_in[1], preferred_element_type=jnp.float32)
            for probs_low, pair_in in zip(low_list, pairs)
        ],
    )
    delta = jnp.einsum("qhgd,qhgd->hgq", grad_out.astype(jnp.float32), attn_out)[..., None]
    value_terms = [
        jnp.einsum("hgqk,qhgd->khd", probs_low, grad_out, preferred_element_type=jnp.float32)
        for probs_low in low_list
    ]
    value_total = (
        shifted(value_terms[reach].astype(jnp.bfloat16), "ctx", -1).astype(jnp.float32)
        + value_terms[0]
    )
    grad_v = value_total.astype(jnp.bfloat16)
    query_terms = []
    key_terms = []
    for pair_in, probs, valid_in in zip(pairs, prob_list, masks):
        dprobs = jnp.einsum(
            "qhgd,khd->hgqk", grad_out, pair_in[1], preferred_element_type=jnp.float32
        )
        dscores = (probs * (dprobs - delta)).astype(jnp.bfloat16)
        q_part = (
            jnp.einsum("hgqk,khd->qhgd", dscores, pair_in[0], preferred_element_type=jnp.float32)
            * scale
        )
        k_part = (
            jnp.einsum(
                "hgqk,qhgd->khd", dscores, rotated_query_rows, preferred_element_type=jnp.float32
            )
            * scale
        )
        query_terms.append(q_part)
        key_terms.append(k_part)
    query_grad = reduce(jnp.add, query_terms)
    key_total = (
        shifted(key_terms[reach].astype(jnp.bfloat16), "ctx", -1).astype(jnp.float32)
        + key_terms[0]
    )
    grad_q = unrotate(query_grad.reshape(tok_rows, head_count, head_dim), cosine, sine).astype(
        jnp.bfloat16
    )
    grad_k = unrotate(key_total, cosine, sine).astype(jnp.bfloat16)
    feats = features[0]
    value_flat = grad_v.reshape(tok_rows, kv_count * head_dim)
    own_rows = param.shape[0]
    n_dp = lax.axis_size("dp")
    piece_rows = own_rows // n_ctx
    spread = ("dp", "ctx")
    feat_cols = lax.all_to_all(
        feats.reshape(tok_rows, n_dp * n_ctx, piece_rows), spread, 1, 0, tiled=False
    )
    value_rows = spread_copy(value_flat, spread)
    pieces = lax.dot_general(
        feat_cols.reshape(-1, piece_rows),
        value_rows.reshape(-1, kv_count * head_dim),
        (((0,), (0,)), ((), ())),
        preferred_element_type=jnp.float32,
    )
    weight_gradient = ring_copy(pieces, "ctx")
    norm_part = jnp.sum(pieces * pieces)
    everyone = ("ctx", "dp", "tp")
    grad_total = spread_sum(norm_part, everyone)
    new_param, new_first, new_second = adam_update(
        param, first_moment_state, second_moment_state, weight_gradient, grad_total
    )
    return (grad_q[None], grad_k[None], grad_v[None], new_param, new_first, new_second)


def solution(mesh):
    placed = (
        P("dp", "ctx", "tp", None),
        P("dp", "ctx", "tp", None),
        P("dp", "ctx", "tp", None),
        P("dp", "ctx", "tp", None),
        P("dp", "ctx", None),
        P("dp", None),
        P(),
        P(),
        P("dp", "tp"),
        P("dp", "tp"),
        P("dp", "tp"),
    )
    return jax.shard_map(
        local_body,
        mesh=mesh,
        in_specs=placed,
        out_specs=(
            P("dp", "ctx", "tp", None),
            P("dp", "ctx", "tp", None),
            P("dp", "ctx", "tp", None),
            P("dp", "tp"),
            P("dp", "tp"),
            P("dp", "tp"),
        ),
        check_vma=False,
    )
```

```python
from functools import reduce
import math

import jax
import jax.numpy as jnp
from jax import lax
from jax.sharding import PartitionSpec as P


ROPE_BASE = 500000.0
NEG_FILL = -1e30
CLIP_NORM = 1000.0
LEARN_RATE = 0.0001
DECAY_RATE = 0.1
BETA_ONE = 0.9
BETA_TWO = 0.95
ADAM_EPS = 1e-08
FIRST_FIX = 1.0 - 0.9**10
SECOND_FIX = 1.0 - 0.95**10


def shifted(array, axis, by):
    peers = lax.axis_size(axis)
    pairs = [(i, i + by) for i in range(peers) if 0 <= i + by < peers]
    return lax.ppermute(array, axis, pairs)


def spread_copy(array, axes):
    peers = lax.axis_size(axes)
    if peers * array.size * array.dtype.itemsize > (4 << 20):
        return lax.all_gather(array, axes, axis=0, tiled=False)
    stacked = jnp.broadcast_to(array[None], (peers,) + array.shape)
    return lax.all_to_all(stacked, axes, 0, 0, tiled=False)


def ring_copy(array, axis):
    peers = lax.axis_size(axis)
    place = lax.axis_index(axis)
    rows = array.shape[0]
    out = jnp.zeros((peers * rows,) + array.shape[1:], array.dtype)
    out = lax.dynamic_update_slice_in_dim(out, array, place * rows, 0)
    for step in range(1, peers):
        moved = lax.ppermute(array, axis, [(i, (i + step) % peers) for i in range(peers)])
        out = lax.dynamic_update_slice_in_dim(out, moved, ((place - step) % peers) * rows, 0)
    return out


def spread_sum(value, axes):
    peers = lax.axis_size(axes)
    if peers > 64:
        return lax.psum(value, axes)
    return jnp.sum(spread_copy(jnp.full((8, 128), value), axes)[:, 0, 0])


def doc_layout(lengths_row, token_index):
    doc_ends = jnp.cumsum(lengths_row)
    passed = doc_ends[None, :] <= token_index[:, None]
    doc_start = jnp.max(jnp.where(passed, doc_ends[None, :], 0), axis=1)
    doc_id = jnp.sum(passed.astype(jnp.int32), axis=1)
    return (doc_id, (token_index - doc_start).astype(jnp.float32))


def rope_tables(position, rope_num, rope_den, head_dim):
    expo = jnp.arange(head_dim // 2, dtype=jnp.float32) * (2.0 / head_dim)
    freq = (
        jnp.exp(-math.log(ROPE_BASE) * expo)
        * rope_den.astype(jnp.float32)
        / rope_num.astype(jnp.float32)
    )
    angle = position[:, None] * freq[None, :]
    cosine = jnp.concatenate([jnp.cos(angle), jnp.cos(angle)], axis=1)
    sine = jnp.concatenate([jnp.sin(angle), jnp.sin(angle)], axis=1)
    return (cosine[:, None, :], sine[:, None, :])


def rotate_low(vectors, cosine, sine):
    half = vectors.shape[-1] // 2
    eye = jnp.eye(half, dtype=jnp.bfloat16)
    zero = jnp.zeros((half, half), jnp.bfloat16)
    swap = jnp.concatenate(
        [jnp.concatenate([zero, eye], axis=1), jnp.concatenate([-eye, zero], axis=1)], axis=0
    )
    turned = jnp.einsum("...d,de->...e", vectors, swap, preferred_element_type=jnp.float32)
    return vectors.astype(jnp.float32) * cosine + turned * sine


def unrotate(grads_in, cosine, sine):
    half = grads_in.shape[-1] // 2
    scaled = grads_in * sine
    turned = jnp.concatenate([scaled[..., half:], -scaled[..., :half]], axis=-1)
    return grads_in * cosine + turned


def adam_update(param, first_moment_state, second_moment_state, weight_gradient, grad_total):
    clip_factor = jnp.minimum(jnp.float32(1.0), CLIP_NORM / jnp.sqrt(grad_total))
    clipped = weight_gradient * clip_factor
    new_first = BETA_ONE * first_moment_state + (1.0 - BETA_ONE) * clipped
    new_second = BETA_TWO * second_moment_state + (1.0 - BETA_TWO) * clipped * clipped
    step_size = new_first / FIRST_FIX / (jnp.sqrt(new_second / SECOND_FIX) + ADAM_EPS)
    new_param = param - LEARN_RATE * (step_size + DECAY_RATE * param)
    return (new_param, new_first, new_second)


def local_body(
    queries,
    keys,
    values,
    output_cotangent,
    features,
    doc_lengths,
    rope_num,
    rope_den,
    param,
    first_moment_state,
    second_moment_state,
):
    tok_rows = queries.shape[1]
    head_count = queries.shape[2]
    head_dim = queries.shape[3]
    kv_count = keys.shape[2]
    group_size = head_count // kv_count
    n_ctx = lax.axis_size("ctx")
    place = lax.axis_index("ctx")
    seq_len = tok_rows * n_ctx
    doc_most = seq_len // 32
    reach = (doc_most + tok_rows - 2) // tok_rows
    scale = head_dim ** (-0.5)
    lengths_row = doc_lengths[0]
    own_index = place * tok_rows + jnp.arange(tok_rows, dtype=jnp.int32)
    own_doc, position = doc_layout(lengths_row, own_index)
    cosine, sine = rope_tables(position, rope_num, rope_den, head_dim)
    rotated_query_rows = rotate_low(queries[0], cosine, sine).astype(jnp.bfloat16)
    rotated_query_rows = rotated_query_rows.reshape(tok_rows, kv_count, group_size, head_dim)
    rotated_key_rows = rotate_low(keys[0], cosine, sine).astype(jnp.bfloat16)
    grad_out = output_cotangent[0].reshape(tok_rows, kv_count, group_size, head_dim)
    kv_pair = jnp.stack([rotated_key_rows, values[0]])
    pairs = [kv_pair]
    offset = 1
    kv_pair = shifted(kv_pair, "ctx", 1)
    pairs.append(kv_pair)
    masks = []
    for offset in range(reach + 1):
        key_index = (place - offset) * tok_rows + jnp.arange(tok_rows, dtype=jnp.int32)
        key_doc = doc_layout(lengths_row, key_index)[0]
        valid = (
            (key_index[None, :] >= 0)
            & (key_index[None, :] <= own_index[:, None])
            & (key_doc[None, :] == own_doc[:, None])
        )
        masks.append(valid)
    score_list = []
    for pair_in, valid_in in zip(pairs, masks):
        raw = (
            jnp.einsum(
                "qhgd,khd->hgqk", rotated_query_rows, pair_in[0], preferred_element_type=jnp.float32
            )
            * scale
        )
        score_list.append(jnp.where(valid_in, raw, NEG_FILL))
    row_top = reduce(
        jnp.maximum, [jnp.max(scores, axis=-1, keepdims=True) for scores in score_list]
    )
    weight_list = [
        jnp.where(valid_in, jnp.exp(scores - row_top), 0.0)
        for scores, valid_in in zip(score_list, masks)
    ]
    row_total = reduce(
        jnp.add, [jnp.sum(weights, axis=-1, keepdims=True) for weights in weight_list]
    )
    prob_list = [weights / row_total for weights in weight_list]
    low_list = [probs.astype(jnp.bfloat16) for probs in prob_list]
    attn_out = reduce(
        jnp.add,
        [
            jnp.einsum("hgqk,khd->qhgd", probs_low, pair_in[1], preferred_element_type=jnp.float32)
            for probs_low, pair_in in zip(low_list, pairs)
        ],
    )
    delta = jnp.einsum("qhgd,qhgd->hgq", grad_out.astype(jnp.float32), attn_out)[..., None]
    value_terms = [
        jnp.einsum("hgqk,qhgd->khd", probs_low, grad_out, preferred_element_type=jnp.float32)
        for probs_low in low_list
    ]
    value_total = (
        shifted(value_terms[reach].astype(jnp.bfloat16), "ctx", -1).astype(jnp.float32)
        + value_terms[0]
    )
    grad_v = value_total.astype(jnp.bfloat16)
    query_terms = []
    key_terms = []
    for pair_in, probs, valid_in in zip(pairs, prob_list, masks):
        dprobs = jnp.einsum(
            "qhgd,khd->hgqk", grad_out, pair_in[1], preferred_element_type=jnp.float32
        )
        dscores = (probs * (dprobs - delta)).astype(jnp.bfloat16)
        q_part = (
            jnp.einsum("hgqk,khd->qhgd", dscores, pair_in[0], preferred_element_type=jnp.float32)
            * scale
        )
        k_part = (
            jnp.einsum(
                "hgqk,qhgd->khd", dscores, rotated_query_rows, preferred_element_type=jnp.float32
            )
            * scale
        )
        query_terms.append(q_part)
        key_terms.append(k_part)
    query_grad = reduce(jnp.add, query_terms)
    key_total = (
        shifted(key_terms[reach].astype(jnp.bfloat16), "ctx", -1).astype(jnp.float32)
        + key_terms[0]
    )
    grad_q = unrotate(query_grad.reshape(tok_rows, head_count, head_dim), cosine, sine).astype(
        jnp.bfloat16
    )
    grad_k = unrotate(key_total, cosine, sine).astype(jnp.bfloat16)
    feats = features[0]
    value_flat = grad_v.reshape(tok_rows, kv_count * head_dim)
    own_rows = param.shape[0]
    n_dp = lax.axis_size("dp")
    piece_rows = own_rows // n_ctx
    spread = ("dp", "ctx")
    feat_cols = lax.all_to_all(
        feats.reshape(tok_rows, n_dp * n_ctx, piece_rows), spread, 1, 0, tiled=False
    )
    if n_dp * n_ctx * 2 * value_flat.size * 2 > (4 << 20):
        value_rows = spread_copy(value_flat, spread)
        pieces = lax.dot_general(
            feat_cols.reshape(-1, piece_rows),
            value_rows.reshape(-1, kv_count * head_dim),
            (((0,), (0,)), ((), ())),
            preferred_element_type=jnp.float32,
        )
    else:
        own_and_back = jnp.stack(
            [value_terms[0].astype(jnp.bfloat16), value_terms[reach].astype(jnp.bfloat16)]
        ).reshape(2, tok_rows, kv_count * head_dim)
        value_rows = spread_copy(own_and_back, spread)
        by_block = feat_cols.reshape(n_dp, n_ctx, tok_rows, piece_rows)
        earlier = jnp.roll(by_block, 1, axis=1)
        feat_pairs = jnp.stack([by_block, earlier], axis=2)
        pieces = lax.dot_general(
            feat_pairs.reshape(-1, piece_rows),
            value_rows.reshape(-1, kv_count * head_dim),
            (((0,), (0,)), ((), ())),
            preferred_element_type=jnp.float32,
        )
    weight_gradient = ring_copy(pieces, "ctx")
    norm_part = jnp.sum(pieces * pieces)
    everyone = ("ctx", "dp", "tp")
    grad_total = spread_sum(norm_part, everyone)
    new_param, new_first, new_second = adam_update(
        param, first_moment_state, second_moment_state, weight_gradient, grad_total
    )
    return (grad_q[None], grad_k[None], grad_v[None], new_param, new_first, new_second)


def solution(mesh):
    placed = (
        P("dp", "ctx", "tp", None),
        P("dp", "ctx", "tp", None),
        P("dp", "ctx", "tp", None),
        P("dp", "ctx", "tp", None),
        P("dp", "ctx", None),
        P("dp", None),
        P(),
        P(),
        P("dp", "tp"),
        P("dp", "tp"),
        P("dp", "tp"),
    )
    return jax.shard_map(
        local_body,
        mesh=mesh,
        in_specs=placed,
        out_specs=(
            P("dp", "ctx", "tp", None),
            P("dp", "ctx", "tp", None),
            P("dp", "ctx", "tp", None),
            P("dp", "tp"),
            P("dp", "tp"),
            P("dp", "tp"),
        ),
        check_vma=False,
    )
```

```python
from functools import reduce
import math

import jax
import jax.numpy as jnp
from jax import lax
from jax.sharding import PartitionSpec as P


ROPE_BASE = 500000.0
NEG_FILL = -1e30
CLIP_NORM = 1000.0
LEARN_RATE = 0.0001
DECAY_RATE = 0.1
BETA_ONE = 0.9
BETA_TWO = 0.95
ADAM_EPS = 1e-08
FIRST_FIX = 1.0 - 0.9**10
SECOND_FIX = 1.0 - 0.95**10


def shifted(array, axis, by):
    peers = lax.axis_size(axis)
    pairs = [(i, i + by) for i in range(peers) if 0 <= i + by < peers]
    return lax.ppermute(array, axis, pairs)


def spread_copy(array, axes):
    peers = lax.axis_size(axes)
    if peers * array.size * array.dtype.itemsize > (4 << 20):
        return lax.all_gather(array, axes, axis=0, tiled=False)
    stacked = jnp.broadcast_to(array[None], (peers,) + array.shape)
    return lax.all_to_all(stacked, axes, 0, 0, tiled=False)


def ring_copy(array, axis):
    peers = lax.axis_size(axis)
    place = lax.axis_index(axis)
    rows = array.shape[0]
    out = jnp.zeros((peers * rows,) + array.shape[1:], array.dtype)
    out = lax.dynamic_update_slice_in_dim(out, array, place * rows, 0)
    for step in range(1, peers):
        moved = lax.ppermute(array, axis, [(i, (i + step) % peers) for i in range(peers)])
        out = lax.dynamic_update_slice_in_dim(out, moved, ((place - step) % peers) * rows, 0)
    return out


def spread_sum(value, axes):
    peers = lax.axis_size(axes)
    if peers > 64:
        return lax.psum(value, axes)
    return jnp.sum(spread_copy(jnp.full((8, 128), value), axes)[:, 0, 0])


def doc_layout(lengths_row, token_index):
    doc_ends = jnp.cumsum(lengths_row)
    passed = doc_ends[None, :] <= token_index[:, None]
    doc_start = jnp.max(jnp.where(passed, doc_ends[None, :], 0), axis=1)
    doc_id = jnp.sum(passed.astype(jnp.int32), axis=1)
    return (doc_id, (token_index - doc_start).astype(jnp.float32))


def rope_tables(position, rope_num, rope_den, head_dim):
    expo = jnp.arange(head_dim // 2, dtype=jnp.float32) * (2.0 / head_dim)
    freq = (
        jnp.exp(-math.log(ROPE_BASE) * expo)
        * rope_den.astype(jnp.float32)
        / rope_num.astype(jnp.float32)
    )
    angle = position[:, None] * freq[None, :]
    cosine = jnp.concatenate([jnp.cos(angle), jnp.cos(angle)], axis=1)
    sine = jnp.concatenate([jnp.sin(angle), jnp.sin(angle)], axis=1)
    return (cosine[:, None, :], sine[:, None, :])


def rotate_low(vectors, cosine, sine):
    half = vectors.shape[-1] // 2
    eye = jnp.eye(half, dtype=jnp.bfloat16)
    zero = jnp.zeros((half, half), jnp.bfloat16)
    swap = jnp.concatenate(
        [jnp.concatenate([zero, eye], axis=1), jnp.concatenate([-eye, zero], axis=1)], axis=0
    )
    turned = jnp.einsum("...d,de->...e", vectors, swap, preferred_element_type=jnp.float32)
    return vectors.astype(jnp.float32) * cosine + turned * sine


def unrotate(grads_in, cosine, sine):
    half = grads_in.shape[-1] // 2
    scaled = grads_in * sine
    turned = jnp.concatenate([scaled[..., half:], -scaled[..., :half]], axis=-1)
    return grads_in * cosine + turned


def adam_update(param, first_moment_state, second_moment_state, weight_gradient, grad_total):
    clip_factor = jnp.minimum(jnp.float32(1.0), CLIP_NORM / jnp.sqrt(grad_total))
    clipped = weight_gradient * clip_factor
    new_first = BETA_ONE * first_moment_state + (1.0 - BETA_ONE) * clipped
    new_second = BETA_TWO * second_moment_state + (1.0 - BETA_TWO) * clipped * clipped
    step_size = new_first / FIRST_FIX / (jnp.sqrt(new_second / SECOND_FIX) + ADAM_EPS)
    new_param = param - LEARN_RATE * (step_size + DECAY_RATE * param)
    return (new_param, new_first, new_second)


def local_body(
    queries,
    keys,
    values,
    output_cotangent,
    features,
    doc_lengths,
    rope_num,
    rope_den,
    param,
    first_moment_state,
    second_moment_state,
):
    tok_rows = queries.shape[1]
    head_count = queries.shape[2]
    head_dim = queries.shape[3]
    kv_count = keys.shape[2]
    group_size = head_count // kv_count
    n_ctx = lax.axis_size("ctx")
    place = lax.axis_index("ctx")
    seq_len = tok_rows * n_ctx
    doc_most = seq_len // 32
    reach = (doc_most + tok_rows - 2) // tok_rows
    scale = head_dim ** (-0.5)
    lengths_row = doc_lengths[0]
    own_index = place * tok_rows + jnp.arange(tok_rows, dtype=jnp.int32)
    own_doc, position = doc_layout(lengths_row, own_index)
    cosine, sine = rope_tables(position, rope_num, rope_den, head_dim)
    rotated_query_rows = rotate_low(queries[0], cosine, sine).astype(jnp.bfloat16)
    rotated_query_rows = rotated_query_rows.reshape(tok_rows, kv_count, group_size, head_dim)
    rotated_key_rows = rotate_low(keys[0], cosine, sine).astype(jnp.bfloat16)
    grad_out = output_cotangent[0].reshape(tok_rows, kv_count, group_size, head_dim)
    kv_pair = jnp.stack([rotated_key_rows, values[0]])
    pairs = [kv_pair]
    offset = 1
    kv_pair = shifted(kv_pair, "ctx", 1)
    pairs.append(kv_pair)
    masks = []
    for offset in range(reach + 1):
        key_index = (place - offset) * tok_rows + jnp.arange(tok_rows, dtype=jnp.int32)
        key_doc = doc_layout(lengths_row, key_index)[0]
        valid = (
            (key_index[None, :] >= 0)
            & (key_index[None, :] <= own_index[:, None])
            & (key_doc[None, :] == own_doc[:, None])
        )
        masks.append(valid)
    score_list = []
    for pair_in, valid_in in zip(pairs, masks):
        raw = (
            jnp.einsum(
                "qhgd,khd->hgqk", rotated_query_rows, pair_in[0], preferred_element_type=jnp.float32
            )
            * scale
        )
        score_list.append(jnp.where(valid_in, raw, NEG_FILL))
    row_top = reduce(
        jnp.maximum, [jnp.max(scores, axis=-1, keepdims=True) for scores in score_list]
    )
    weight_list = [
        jnp.where(valid_in, jnp.exp(scores - row_top), 0.0)
        for scores, valid_in in zip(score_list, masks)
    ]
    row_total = reduce(
        jnp.add, [jnp.sum(weights, axis=-1, keepdims=True) for weights in weight_list]
    )
    prob_list = [weights / row_total for weights in weight_list]
    low_list = [probs.astype(jnp.bfloat16) for probs in prob_list]
    attn_out = reduce(
        jnp.add,
        [
            jnp.einsum("hgqk,khd->qhgd", probs_low, pair_in[1], preferred_element_type=jnp.float32)
            for probs_low, pair_in in zip(low_list, pairs)
        ],
    )
    delta = jnp.einsum("qhgd,qhgd->hgq", grad_out.astype(jnp.float32), attn_out)[..., None]
    value_terms = [
        jnp.einsum("hgqk,qhgd->khd", probs_low, grad_out, preferred_element_type=jnp.float32)
        for probs_low in low_list
    ]
    value_total = (
        shifted(value_terms[reach].astype(jnp.bfloat16), "ctx", -1).astype(jnp.float32)
        + value_terms[0]
    )
    grad_v = value_total.astype(jnp.bfloat16)
    query_terms = []
    key_terms = []
    for pair_in, probs, valid_in in zip(pairs, prob_list, masks):
        dprobs = jnp.einsum(
            "qhgd,khd->hgqk", grad_out, pair_in[1], preferred_element_type=jnp.float32
        )
        dscores = (probs * (dprobs - delta)).astype(jnp.bfloat16)
        q_part = (
            jnp.einsum("hgqk,khd->qhgd", dscores, pair_in[0], preferred_element_type=jnp.float32)
            * scale
        )
        k_part = (
            jnp.einsum(
                "hgqk,qhgd->khd", dscores, rotated_query_rows, preferred_element_type=jnp.float32
            )
            * scale
        )
        query_terms.append(q_part)
        key_terms.append(k_part)
    query_grad = reduce(jnp.add, query_terms)
    key_total = (
        shifted(key_terms[reach].astype(jnp.bfloat16), "ctx", -1).astype(jnp.float32)
        + key_terms[0]
    )
    grad_q = unrotate(query_grad.reshape(tok_rows, head_count, head_dim), cosine, sine).astype(
        jnp.bfloat16
    )
    grad_k = unrotate(key_total, cosine, sine).astype(jnp.bfloat16)
    feats = features[0]
    value_flat = grad_v.reshape(tok_rows, kv_count * head_dim)
    own_rows = param.shape[0]
    n_dp = lax.axis_size("dp")
    piece_rows = own_rows // n_ctx
    spread = ("dp", "ctx")
    n_tp = lax.axis_size("tp")
    core = lax.axis_index("tp")
    split_cols = n_tp == 2 and piece_rows % 2 == 0
    if split_cols:
        halves = feats.reshape(tok_rows, n_dp * n_ctx, 2, piece_rows // 2)
        mine = lax.dynamic_index_in_dim(halves, core, axis=2, keepdims=False)
    else:
        mine = feats.reshape(tok_rows, n_dp * n_ctx, piece_rows)
    feat_cols = lax.all_to_all(mine, spread, 1, 0, tiled=False)
    if split_cols:
        other = lax.ppermute(feat_cols, "tp", [(0, 1), (1, 0)])
        feat_cols = jnp.where(
            core == 0,
            jnp.concatenate([feat_cols, other], axis=-1),
            jnp.concatenate([other, feat_cols], axis=-1),
        )
    value_rows = spread_copy(value_flat, spread)
    pieces = lax.dot_general(
        feat_cols.reshape(-1, piece_rows),
        value_rows.reshape(-1, kv_count * head_dim),
        (((0,), (0,)), ((), ())),
        preferred_element_type=jnp.float32,
    )
    weight_gradient = ring_copy(pieces, "ctx")
    norm_part = jnp.sum(pieces * pieces)
    everyone = ("ctx", "dp", "tp")
    grad_total = spread_sum(norm_part, everyone)
    new_param, new_first, new_second = adam_update(
        param, first_moment_state, second_moment_state, weight_gradient, grad_total
    )
    return (grad_q[None], grad_k[None], grad_v[None], new_param, new_first, new_second)


def solution(mesh):
    placed = (
        P("dp", "ctx", "tp", None),
        P("dp", "ctx", "tp", None),
        P("dp", "ctx", "tp", None),
        P("dp", "ctx", "tp", None),
        P("dp", "ctx", None),
        P("dp", None),
        P(),
        P(),
        P("dp", "tp"),
        P("dp", "tp"),
        P("dp", "tp"),
    )
    return jax.shard_map(
        local_body,
        mesh=mesh,
        in_specs=placed,
        out_specs=(
            P("dp", "ctx", "tp", None),
            P("dp", "ctx", "tp", None),
            P("dp", "ctx", "tp", None),
            P("dp", "tp"),
            P("dp", "tp"),
            P("dp", "tp"),
        ),
        check_vma=False,
    )
```

```python
from functools import reduce
import math

import jax
import jax.numpy as jnp
from jax import lax
from jax.sharding import PartitionSpec as P


ROPE_BASE = 500000.0
NEG_FILL = -1e30
CLIP_NORM = 1000.0
LEARN_RATE = 0.0001
DECAY_RATE = 0.1
BETA_ONE = 0.9
BETA_TWO = 0.95
ADAM_EPS = 1e-08
FIRST_FIX = 1.0 - 0.9**10
SECOND_FIX = 1.0 - 0.95**10


def shifted(array, axis, by):
    peers = lax.axis_size(axis)
    pairs = [(i, i + by) for i in range(peers) if 0 <= i + by < peers]
    return lax.ppermute(array, axis, pairs)


def spread_copy(array, axes):
    peers = lax.axis_size(axes)
    if peers * array.size * array.dtype.itemsize > (4 << 20):
        return lax.all_gather(array, axes, axis=0, tiled=False)
    stacked = jnp.broadcast_to(array[None], (peers,) + array.shape)
    return lax.all_to_all(stacked, axes, 0, 0, tiled=False)


def ring_copy(array, axis):
    peers = lax.axis_size(axis)
    place = lax.axis_index(axis)
    rows = array.shape[0]
    out = jnp.zeros((peers * rows,) + array.shape[1:], array.dtype)
    out = lax.dynamic_update_slice_in_dim(out, array, place * rows, 0)
    for step in range(1, peers):
        moved = lax.ppermute(array, axis, [(i, (i + step) % peers) for i in range(peers)])
        out = lax.dynamic_update_slice_in_dim(out, moved, ((place - step) % peers) * rows, 0)
    return out


def spread_sum(value, axes):
    peers = lax.axis_size(axes)
    if peers > 64:
        return lax.psum(value, axes)
    return jnp.sum(spread_copy(jnp.full((8, 128), value), axes)[:, 0, 0])


def doc_layout(lengths_row, token_index):
    doc_ends = jnp.cumsum(lengths_row)
    passed = doc_ends[None, :] <= token_index[:, None]
    doc_start = jnp.max(jnp.where(passed, doc_ends[None, :], 0), axis=1)
    doc_id = jnp.sum(passed.astype(jnp.int32), axis=1)
    return (doc_id, (token_index - doc_start).astype(jnp.float32))


def rope_tables(position, rope_num, rope_den, head_dim):
    expo = jnp.arange(head_dim // 2, dtype=jnp.float32) * (2.0 / head_dim)
    freq = (
        jnp.exp(-math.log(ROPE_BASE) * expo)
        * rope_den.astype(jnp.float32)
        / rope_num.astype(jnp.float32)
    )
    angle = position[:, None] * freq[None, :]
    cosine = jnp.concatenate([jnp.cos(angle), jnp.cos(angle)], axis=1)
    sine = jnp.concatenate([jnp.sin(angle), jnp.sin(angle)], axis=1)
    return (cosine[:, None, :], sine[:, None, :])


def rotate_low(vectors, cosine, sine):
    half = vectors.shape[-1] // 2
    eye = jnp.eye(half, dtype=jnp.bfloat16)
    zero = jnp.zeros((half, half), jnp.bfloat16)
    swap = jnp.concatenate(
        [jnp.concatenate([zero, eye], axis=1), jnp.concatenate([-eye, zero], axis=1)], axis=0
    )
    turned = jnp.einsum("...d,de->...e", vectors, swap, preferred_element_type=jnp.float32)
    return vectors.astype(jnp.float32) * cosine + turned * sine


def unrotate(grads_in, cosine, sine):
    half = grads_in.shape[-1] // 2
    scaled = grads_in * sine
    turned = jnp.concatenate([scaled[..., half:], -scaled[..., :half]], axis=-1)
    return grads_in * cosine + turned


def adam_update(param, first_moment_state, second_moment_state, weight_gradient, grad_total):
    clip_factor = jnp.minimum(jnp.float32(1.0), CLIP_NORM / jnp.sqrt(grad_total))
    clipped = weight_gradient * clip_factor
    new_first = BETA_ONE * first_moment_state + (1.0 - BETA_ONE) * clipped
    new_second = BETA_TWO * second_moment_state + (1.0 - BETA_TWO) * clipped * clipped
    step_size = new_first / FIRST_FIX / (jnp.sqrt(new_second / SECOND_FIX) + ADAM_EPS)
    new_param = param - LEARN_RATE * (step_size + DECAY_RATE * param)
    return (new_param, new_first, new_second)


def local_body(
    queries,
    keys,
    values,
    output_cotangent,
    features,
    doc_lengths,
    rope_num,
    rope_den,
    param,
    first_moment_state,
    second_moment_state,
):
    tok_rows = queries.shape[1]
    head_count = queries.shape[2]
    head_dim = queries.shape[3]
    kv_count = keys.shape[2]
    group_size = head_count // kv_count
    n_ctx = lax.axis_size("ctx")
    place = lax.axis_index("ctx")
    seq_len = tok_rows * n_ctx
    doc_most = seq_len // 32
    reach = (doc_most + tok_rows - 2) // tok_rows
    scale = head_dim ** (-0.5)
    lengths_row = doc_lengths[0]
    own_index = place * tok_rows + jnp.arange(tok_rows, dtype=jnp.int32)
    own_doc, position = doc_layout(lengths_row, own_index)
    cosine, sine = rope_tables(position, rope_num, rope_den, head_dim)
    rotated_query_rows = rotate_low(queries[0], cosine, sine).astype(jnp.bfloat16)
    rotated_query_rows = rotated_query_rows.reshape(tok_rows, kv_count, group_size, head_dim)
    rotated_key_rows = rotate_low(keys[0], cosine, sine).astype(jnp.bfloat16)
    grad_out = output_cotangent[0].reshape(tok_rows, kv_count, group_size, head_dim)
    kv_pair = jnp.stack([rotated_key_rows, values[0]])
    pairs = [kv_pair]
    offset = 1
    kv_pair = shifted(kv_pair, "ctx", 1)
    pairs.append(kv_pair)
    masks = []
    for offset in range(reach + 1):
        key_index = (place - offset) * tok_rows + jnp.arange(tok_rows, dtype=jnp.int32)
        key_doc = doc_layout(lengths_row, key_index)[0]
        valid = (
            (key_index[None, :] >= 0)
            & (key_index[None, :] <= own_index[:, None])
            & (key_doc[None, :] == own_doc[:, None])
        )
        masks.append(valid)
    score_list = []
    for pair_in, valid_in in zip(pairs, masks):
        raw = (
            jnp.einsum(
                "qhgd,khd->hgqk", rotated_query_rows, pair_in[0], preferred_element_type=jnp.float32
            )
            * scale
        )
        score_list.append(jnp.where(valid_in, raw, NEG_FILL))
    row_top = reduce(
        jnp.maximum, [jnp.max(scores, axis=-1, keepdims=True) for scores in score_list]
    )
    weight_list = [
        jnp.where(valid_in, jnp.exp(scores - row_top), 0.0)
        for scores, valid_in in zip(score_list, masks)
    ]
    row_total = reduce(
        jnp.add, [jnp.sum(weights, axis=-1, keepdims=True) for weights in weight_list]
    )
    prob_list = [weights / row_total for weights in weight_list]
    low_list = [probs.astype(jnp.bfloat16) for probs in prob_list]
    attn_out = reduce(
        jnp.add,
        [
            jnp.einsum("hgqk,khd->qhgd", probs_low, pair_in[1], preferred_element_type=jnp.float32)
            for probs_low, pair_in in zip(low_list, pairs)
        ],
    )
    delta = jnp.einsum("qhgd,qhgd->hgq", grad_out.astype(jnp.float32), attn_out)[..., None]
    value_terms = [
        jnp.einsum("hgqk,qhgd->khd", probs_low, grad_out, preferred_element_type=jnp.float32)
        for probs_low in low_list
    ]
    value_total = (
        shifted(value_terms[reach].astype(jnp.bfloat16), "ctx", -1).astype(jnp.float32)
        + value_terms[0]
    )
    grad_v = value_total.astype(jnp.bfloat16)
    query_terms = []
    key_terms = []
    for pair_in, probs, valid_in in zip(pairs, prob_list, masks):
        dprobs = jnp.einsum(
            "qhgd,khd->hgqk", grad_out, pair_in[1], preferred_element_type=jnp.float32
        )
        dscores = (probs * (dprobs - delta)).astype(jnp.bfloat16)
        q_part = (
            jnp.einsum("hgqk,khd->qhgd", dscores, pair_in[0], preferred_element_type=jnp.float32)
            * scale
        )
        k_part = (
            jnp.einsum(
                "hgqk,qhgd->khd", dscores, rotated_query_rows, preferred_element_type=jnp.float32
            )
            * scale
        )
        query_terms.append(q_part)
        key_terms.append(k_part)
    query_grad = reduce(jnp.add, query_terms)
    key_total = (
        shifted(key_terms[reach].astype(jnp.bfloat16), "ctx", -1).astype(jnp.float32)
        + key_terms[0]
    )
    grad_q = unrotate(query_grad.reshape(tok_rows, head_count, head_dim), cosine, sine).astype(
        jnp.bfloat16
    )
    grad_k = unrotate(key_total, cosine, sine).astype(jnp.bfloat16)
    feats = features[0]
    value_flat = grad_v.reshape(tok_rows, kv_count * head_dim)
    own_rows = param.shape[0]
    n_dp = lax.axis_size("dp")
    piece_rows = own_rows // n_ctx
    spread = ("ctx", "dp")
    by_place = feats.reshape(tok_rows, n_dp, n_ctx, piece_rows).transpose(0, 2, 1, 3)
    feat_cols = lax.all_to_all(
        by_place.reshape(tok_rows, n_dp * n_ctx, piece_rows), spread, 1, 0, tiled=False
    )
    value_rows = spread_copy(value_flat, spread)
    pieces = lax.dot_general(
        feat_cols.reshape(-1, piece_rows),
        value_rows.reshape(-1, kv_count * head_dim),
        (((0,), (0,)), ((), ())),
        preferred_element_type=jnp.float32,
    )
    weight_gradient = ring_copy(pieces, "ctx")
    norm_part = jnp.sum(pieces * pieces)
    everyone = ("ctx", "dp", "tp")
    grad_total = spread_sum(norm_part, everyone)
    new_param, new_first, new_second = adam_update(
        param, first_moment_state, second_moment_state, weight_gradient, grad_total
    )
    return (grad_q[None], grad_k[None], grad_v[None], new_param, new_first, new_second)


def solution(mesh):
    placed = (
        P("dp", "ctx", "tp", None),
        P("dp", "ctx", "tp", None),
        P("dp", "ctx", "tp", None),
        P("dp", "ctx", "tp", None),
        P("dp", "ctx", None),
        P("dp", None),
        P(),
        P(),
        P("dp", "tp"),
        P("dp", "tp"),
        P("dp", "tp"),
    )
    return jax.shard_map(
        local_body,
        mesh=mesh,
        in_specs=placed,
        out_specs=(
            P("dp", "ctx", "tp", None),
            P("dp", "ctx", "tp", None),
            P("dp", "ctx", "tp", None),
            P("dp", "tp"),
            P("dp", "tp"),
            P("dp", "tp"),
        ),
        check_vma=False,
    )
```
